32 devices in a mesh: parts: 2 (over y), user: 16 (over z, x, core).
Axes of the slice: x: 2, y: 2, z: 4, core: 2. Of those that a mesh axis runs over, the one named last changes fastest.
Arguments:
- counts: int32 [1024, 16384], P(None, ('parts', 'user')), parts along dimension 1, may hold values from 0 to 3
- first_bin: int32 [16384], P(('parts', 'user')), parts along dimension 0, may hold values from 0 to 511
- time_factor: float32 [2048, 128], P('parts'), parts along dimension 0, may hold values from -6 to 6
- user_factor: float32 [16384, 128], P(('parts', 'user')), parts along dimension 0, may hold values from -0.5 to 0.5
- user_base: float32 [16384], P(('parts', 'user')), parts along dimension 0, may hold values from -4 to 4
Outputs:
- new_time_factor: float32 [2048, 128], P(('parts', 'user')), parts along dimension 0
- new_user_factor: float32 [16384, 128], P(('parts', 'user')), parts along dimension 0
The draws below stay inside these ranges and needn't reach their ends.
There are 2 independent parts, one for each index of `parts`. The reference program is written for one: setup_inputs(seed, part) draws one part's arguments, and reference() takes and returns one part's arrays. A program takes and returns all parts, laid end to end along the dimension named above; each array names one. Nothing has to cross between parts.
All inputs are finite; a program needn't handle non-finite values.
Results may differ from the reference program's by a relative error of at most 0.0003.
Values sent between devices are 32-bit elements; how exact they have to be, the bound alone decides.
No kernel may reach another device: no remote copies, remote signals or barrier semaphores. Data moves between devices by JAX's collectives and lax.ppermute only.
A program may use at most 64 MiB of HBM per device.

```python
import jax
import jax.numpy as jnp
from jax import lax

R = 128
TIME = 1024
USER_DEV = 512
SWEEPS = 2
USERS = 8192
N_USER = 16


def plant(array, own_key, smallest, top_value):
    longest = array.shape.index(max(array.shape))
    spots = []
    for shift in (0, 1):
        where = [jax.random.randint(jax.random.fold_in(own_key, axis), (), 0, length) for axis, length in enumerate(array.shape)]
        where[longest] = (where[longest] + shift) % array.shape[longest]
        spots.append(tuple(where))
    return array.at[spots[0]].set(smallest).at[spots[1]].set(top_value)


def steps_of(stream_key, shape, shards, low, largest):
    def one(axis_at, blocks):
        steps = jax.random.uniform(jax.random.fold_in(jax.random.fold_in(stream_key, 6), axis_at), (blocks,), jnp.float32, low / len(shards), largest / len(shards))
        return jnp.repeat(jnp.exp(steps), shape[axis_at] // blocks).reshape((-1,) + (1,) * (len(shape) - axis_at - 1))

    factor_of = one(*shards[0])
    for cut in shards[1:]:
        factor_of = factor_of * one(*cut)
    return factor_of


def normal_values(key, dims, deviation, limit, split=(), kind=jnp.bfloat16):
    gain = steps_of(key, dims, split, -0.22, 0.18) if split else 1.0
    array = jax.random.normal(key, dims, jnp.float32) * deviation * gain
    return jnp.minimum(jnp.maximum(array, -limit), limit).astype(kind)


def setup_inputs(seed: int = 0, part: int = 0) -> dict:
    key_list = jax.random.split(jax.random.key(seed), 6)
    part_splits = jax.random.split(jax.random.fold_in(key_list[5], part), 6)
    return {
        "counts": plant(jax.random.randint(part_splits[0], (TIME, USERS), 0, 4), jax.random.fold_in(part_splits[0], 1), 0, 3).astype(jnp.int32),
        "first_bin": plant(jax.random.randint(part_splits[1], (USERS,), 0, TIME // 2), jax.random.fold_in(part_splits[1], 1), 0, (TIME // 2) - 1).astype(jnp.int32),
        "time_factor": normal_values(part_splits[2], (TIME, R), 1.0, 6.0, (), jnp.float32),
        "user_factor": normal_values(part_splits[3], (USERS, R), R ** -0.5, 0.5, ((0, 16),), jnp.float32),
        "user_base": normal_values(part_splits[4], (USERS,), 1.0, 4.0, ((0, 16),), jnp.float32),
    }


damping = 0.5
background = 0.5


def product(left, right):
    return jnp.dot(left, right, precision=lax.Precision.HIGHEST, preferred_element_type=jnp.float32)


def local_terms(time_factor, user_block, base_block, count_block, start_block):
    linear = product(time_factor, user_block.T) + base_block[None, :]
    time_bins = jnp.arange(time_factor.shape[0], dtype=jnp.int32)[:, None]
    observed = (time_bins >= start_block[None, :]).astype(jnp.float32)
    intensity = jax.nn.softplus(linear) + background
    gate_value = jax.nn.sigmoid(linear)
    residual = observed * gate_value * (1.0 - count_block.astype(jnp.float32) / intensity)
    curvature = observed * gate_value * gate_value / intensity
    return residual, curvature


def reference(counts, first_bin, time_factor, user_factor, user_base):
    indices = jnp.arange(N_USER, dtype=jnp.int32)

    def block_of(user_matrix, block_index):
        begin = (block_index * USER_DEV).astype(jnp.int32)
        return lax.dynamic_slice_in_dim(user_matrix, begin, USER_DEV, 0)

    def inputs_of(block_index):
        begin = (block_index * USER_DEV).astype(jnp.int32)
        return (lax.dynamic_slice_in_dim(user_base, begin, USER_DEV, 0),
                lax.dynamic_slice_in_dim(counts, begin, USER_DEV, 1),
                lax.dynamic_slice_in_dim(first_bin, begin, USER_DEV, 0))

    for sweep in range(SWEEPS):
        def first_pass(block_index):
            base_block, count_block, start_block = inputs_of(block_index)
            user_block = block_of(user_factor, block_index)
            residual, curvature = local_terms(time_factor, user_block, base_block, count_block, start_block)
            return product(residual.T, time_factor), product(residual, user_block)

        grad_blocks, time_terms = lax.map(first_pass, indices)
        grad_time = jnp.sum(time_terms, axis=0)
        grad_user = grad_blocks.reshape(USERS, R)
        norm_total = jnp.sum(grad_time * grad_time) + jnp.sum(grad_user * grad_user)

        def second_pass(block_index):
            base_block, count_block, start_block = inputs_of(block_index)
            user_block = block_of(user_factor, block_index)
            grad_block = block_of(grad_user, block_index)
            residual, curvature = local_terms(time_factor, user_block, base_block, count_block, start_block)
            tangent_image = product(grad_time, user_block.T) + product(time_factor, grad_block.T)
            return jnp.sum(curvature * tangent_image * tangent_image)

        bending = jnp.sum(lax.map(second_pass, indices))
        relax_step = norm_total / (bending + damping * norm_total)
        time_factor = time_factor - relax_step * grad_time
        user_factor = user_factor - relax_step * grad_user
    return time_factor, user_factor
```

```python
import jax
import jax.numpy as jnp
from jax import lax
from jax.sharding import PartitionSpec as P

SWEEPS = 2


damping = 0.5
background = 0.5


def product(left, right):
    return jnp.dot(left, right, precision=lax.Precision.HIGHEST, preferred_element_type=jnp.float32)


def local_terms(time_factor, user_block, base_block, count_block, start_block):
    linear = product(time_factor, user_block.T) + base_block[None, :]
    time_bins = jnp.arange(time_factor.shape[0], dtype=jnp.int32)[:, None]
    observed = (time_bins >= start_block[None, :]).astype(jnp.float32)
    intensity = jax.nn.softplus(linear) + background
    gate_value = jax.nn.sigmoid(linear)
    residual = observed * gate_value * (1.0 - count_block.astype(jnp.float32) / intensity)
    curvature = observed * gate_value * gate_value / intensity
    return (residual, curvature)


def exchange(value, n, distance):
    return lax.ppermute(value, "user", [(i, i ^ distance) for i in range(n)])


def sum_over_users(partial, n):
    if n == 1:
        return partial
    if n & (n - 1) or partial.shape[0] % n:
        return lax.psum(partial, "user")
    me = lax.axis_index("user")
    distances = []
    d = 1
    while d < n:
        distances.append(d)
        d *= 2
    block = partial
    for d in distances:
        half = block.shape[0] // 2
        upper = (me // d) % 2
        keep = lax.dynamic_slice_in_dim(block, upper * half, half, 0)
        send = lax.dynamic_slice_in_dim(block, (1 - upper) * half, half, 0)
        block = keep + exchange(send, n, d)
    for d in reversed(distances):
        other = exchange(block, n, d)
        upper = (me // d) % 2
        both = jnp.concatenate([block, other], axis=0)
        swapped = jnp.concatenate([other, block], axis=0)
        block = jnp.where(upper == 0, both, swapped)
    return block


def sum_scalars(values, n):
    lanes = jnp.zeros((1, 128), jnp.float32)
    for k, v in enumerate(values):
        lanes = lanes.at[0, k].set(v)
    if n == 1:
        total = lanes[0]
    else:
        spread = jnp.broadcast_to(lanes[None], (n, 1, 128))
        total = jnp.sum(lax.all_to_all(spread, "user", 0, 0, tiled=False), axis=(0, 1))
    return [total[k] for k in range(len(values))]


def body(n, counts, first_bin, time_factor, user_factor, user_base):
    shard_rows = time_factor.shape[0] // n
    offset = lax.axis_index("user") * shard_rows
    mine_rows = time_factor
    for sweep in range(SWEEPS):
        residual, curvature = local_terms(time_factor, user_factor, user_base, counts, first_bin)
        grad_user = product(residual.T, time_factor)
        grad_whole = sum_over_users(product(residual, user_factor), n)
        user_norm = jnp.sum(grad_user * grad_user)
        tangent_image = product(grad_whole, user_factor.T) + product(time_factor, grad_user.T)
        bending = jnp.sum(curvature * tangent_image * tangent_image)
        user_norm_total, bend_total = sum_scalars([user_norm, bending], n)
        norm_total = jnp.sum(grad_whole * grad_whole) + user_norm_total
        relax_step = norm_total / (bend_total + damping * norm_total)
        user_factor = user_factor - relax_step * grad_user
        if sweep + 1 < SWEEPS:
            time_factor = time_factor - relax_step * grad_whole
        else:
            mine_rows = lax.dynamic_slice_in_dim(
                time_factor - relax_step * grad_whole, offset, shard_rows, 0
            )
    return (mine_rows, user_factor)


def solution(mesh):
    n = mesh.shape["user"]
    return jax.shard_map(
        lambda *args: body(n, *args),
        mesh=mesh,
        in_specs=(
            P(None, ("parts", "user")),
            P(("parts", "user")),
            P("parts", None),
            P(("parts", "user"), None),
            P(("parts", "user")),
        ),
        out_specs=(P(("parts", "user"), None), P(("parts", "user"), None)),
        check_vma=False,
    )
```

```python
import jax
import jax.numpy as jnp
from jax import lax
from jax.sharding import PartitionSpec as P

SWEEPS = 2


damping = 0.5
background = 0.5


def product(left, right):
    return jnp.dot(left, right, precision=lax.Precision.HIGHEST, preferred_element_type=jnp.float32)


def local_terms(time_factor, user_block, base_block, count_block, start_block):
    linear = product(time_factor, user_block.T) + base_block[None, :]
    time_bins = jnp.arange(time_factor.shape[0], dtype=jnp.int32)[:, None]
    observed = time_bins >= start_block[None, :]
    decay = jnp.exp(-jnp.abs(linear))
    intensity = jnp.maximum(linear, 0.0) + jnp.log1p(decay) + background
    gate_value = jnp.where(linear >= 0, 1.0, decay) / (1.0 + decay)
    inverse = 1.0 / intensity
    residual = jnp.where(observed, gate_value * (1.0 - count_block.astype(jnp.float32) * inverse), 0.0)
    curvature = jnp.where(observed, gate_value * gate_value * inverse, 0.0)
    return (residual, curvature)


def exchange(value, n, distance):
    return lax.ppermute(value, "user", [(i, i ^ distance) for i in range(n)])


def sum_over_users(partial, n):
    if n == 1:
        return partial
    if n & (n - 1) or partial.shape[0] % n:
        return lax.psum(partial, "user")
    me = lax.axis_index("user")
    distances = []
    d = 1
    while d < n:
        distances.append(d)
        d *= 2
    block = partial
    for d in distances:
        half = block.shape[0] // 2
        upper = (me // d) % 2
        keep = lax.dynamic_slice_in_dim(block, upper * half, half, 0)
        send = lax.dynamic_slice_in_dim(block, (1 - upper) * half, half, 0)
        block = keep + exchange(send, n, d)
    for d in reversed(distances):
        other = exchange(block, n, d)
        upper = (me // d) % 2
        both = jnp.concatenate([block, other], axis=0)
        swapped = jnp.concatenate([other, block], axis=0)
        block = jnp.where(upper == 0, both, swapped)
    return block


def sum_scalars(values, n):
    lane = lax.broadcasted_iota(jnp.int32, (n, 1, 128), 2)
    spread = jnp.zeros((n, 1, 128), jnp.float32)
    for k, v in enumerate(values):
        spread = jnp.where(lane == k, v, spread)
    if n > 1:
        spread = lax.all_to_all(spread, "user", 0, 0, tiled=False)
    total = jnp.sum(spread, axis=(0, 1))
    return [total[k] for k in range(len(values))]


def body(n, counts, first_bin, time_factor, user_factor, user_base):
    shard_rows = time_factor.shape[0] // n
    offset = lax.axis_index("user") * shard_rows
    mine_rows = time_factor
    for sweep in range(SWEEPS):
        residual, curvature = local_terms(time_factor, user_factor, user_base, counts, first_bin)
        grad_user = product(residual.T, time_factor)
        grad_whole = sum_over_users(product(residual, user_factor), n)
        user_norm = jnp.sum(grad_user * grad_user)
        tangent_image = product(grad_whole, user_factor.T) + product(time_factor, grad_user.T)
        bending = jnp.sum(curvature * tangent_image * tangent_image)
        user_norm_total, bend_total = sum_scalars([user_norm, bending], n)
        norm_total = jnp.sum(grad_whole * grad_whole) + user_norm_total
        relax_step = norm_total / (bend_total + damping * norm_total)
        user_factor = user_factor - relax_step * grad_user
        if sweep + 1 < SWEEPS:
            time_factor = time_factor - relax_step * grad_whole
        else:
            mine_rows = lax.dynamic_slice_in_dim(
                time_factor - relax_step * grad_whole, offset, shard_rows, 0
            )
    return (mine_rows, user_factor)


def solution(mesh):
    n = mesh.shape["user"]
    return jax.shard_map(
        lambda *args: body(n, *args),
        mesh=mesh,
        in_specs=(
            P(None, ("parts", "user")),
            P(("parts", "user")),
            P("parts", None),
            P(("parts", "user"), None),
            P(("parts", "user")),
        ),
        out_specs=(P(("parts", "user"), None), P(("parts", "user"), None)),
        check_vma=False,
    )
```

```python
import jax
import jax.numpy as jnp
from jax import lax
from jax.sharding import PartitionSpec as P

SWEEPS = 2


damping = 0.5
background = 0.5


def product(left, right):
    return jnp.dot(left, right, precision=lax.Precision.HIGHEST, preferred_element_type=jnp.float32)


def local_terms(time_factor, user_block, base_block, count_block, start_block):
    linear = product(time_factor, user_block.T) + base_block[None, :]
    time_bins = jnp.arange(time_factor.shape[0], dtype=jnp.int32)[:, None]
    observed = time_bins >= start_block[None, :]
    decay = jnp.exp(-jnp.abs(linear))
    intensity = jnp.maximum(linear, 0.0) + jnp.log1p(decay) + background
    gate_value = jnp.where(linear >= 0, 1.0, decay) / (1.0 + decay)
    inverse = 1.0 / intensity
    residual = jnp.where(observed, gate_value * (1.0 - count_block.astype(jnp.float32) * inverse), 0.0)
    curvature = jnp.where(observed, gate_value * gate_value * inverse, 0.0)
    return (residual, curvature)


def exchange(value, n, distance):
    return lax.ppermute(value, "user", [(i, i ^ distance) for i in range(n)])


def sum_over_users(partial, n):
    if n == 1:
        return partial, [(partial, 0)]
    if n & (n - 1) or partial.shape[0] % n:
        total = lax.psum(partial, "user")
        return total, [(total, 0)]
    me = lax.axis_index("user")
    distances = []
    d = 1
    while d < n:
        distances.append(d)
        d *= 2
    halving, butterfly = distances[:2], distances[2:]
    block, offset = partial, 0
    for d in halving:
        half = block.shape[0] // 2
        upper = (me // d) % 2
        keep = lax.dynamic_slice_in_dim(block, upper * half, half, 0)
        send = lax.dynamic_slice_in_dim(block, (1 - upper) * half, half, 0)
        offset = offset + upper * half
        block = keep + exchange(send, n, d)
    for d in butterfly:
        block = block + exchange(block, n, d)
    pieces = [(block, offset)]
    for d in reversed(halving):
        rows = block.shape[0]
        other = exchange(block, n, d)
        upper = (me // d) % 2
        pieces.append((other, offset + (1 - 2 * upper) * rows))
        both = jnp.concatenate([block, other], axis=0)
        swapped = jnp.concatenate([other, block], axis=0)
        block = jnp.where(upper == 0, both, swapped)
        offset = offset - upper * rows
    return block, pieces


def sum_scalars(values, n):
    lane = lax.broadcasted_iota(jnp.int32, (n, 1, 128), 2)
    spread = jnp.zeros((n, 1, 128), jnp.float32)
    for k, v in enumerate(values):
        spread = jnp.where(lane == k, v, spread)
    if n > 1:
        spread = lax.all_to_all(spread, "user", 0, 0, tiled=False)
    total = jnp.sum(spread, axis=(0, 1))
    return [total[k] for k in range(len(values))]


def body(n, counts, first_bin, time_factor, user_factor, user_base):
    shard_rows = time_factor.shape[0] // n
    offset = lax.axis_index("user") * shard_rows
    mine_rows = time_factor
    for sweep in range(SWEEPS):
        residual, curvature = local_terms(time_factor, user_factor, user_base, counts, first_bin)
        grad_user = product(residual.T, time_factor)
        grad_whole, pieces = sum_over_users(product(residual, user_factor), n)
        user_norm = jnp.sum(grad_user * grad_user)
        bending = 0.0
        for piece, first in pieces:
            rows = piece.shape[0]
            tangent_image = product(piece, user_factor.T) + product(
                lax.dynamic_slice_in_dim(time_factor, first, rows, 0), grad_user.T
            )
            weight = lax.dynamic_slice_in_dim(curvature, first, rows, 0)
            bending = bending + jnp.sum(weight * tangent_image * tangent_image)
        user_norm_total, bend_total = sum_scalars([user_norm, bending], n)
        norm_total = jnp.sum(grad_whole * grad_whole) + user_norm_total
        relax_step = norm_total / (bend_total + damping * norm_total)
        user_factor = user_factor - relax_step * grad_user
        if sweep + 1 < SWEEPS:
            time_factor = time_factor - relax_step * grad_whole
        else:
            mine_rows = lax.dynamic_slice_in_dim(
                time_factor - relax_step * grad_whole, offset, shard_rows, 0
            )
    return (mine_rows, user_factor)


def solution(mesh):
    n = mesh.shape["user"]
    return jax.shard_map(
        lambda *args: body(n, *args),
        mesh=mesh,
        in_specs=(
            P(None, ("parts", "user")),
            P(("parts", "user")),
            P("parts", None),
            P(("parts", "user"), None),
            P(("parts", "user")),
        ),
        out_specs=(P(("parts", "user"), None), P(("parts", "user"), None)),
        check_vma=False,
    )
```

```python
import jax
import jax.numpy as jnp
from jax import lax
from jax.sharding import PartitionSpec as P

SWEEPS = 2


damping = 0.5
background = 0.5


def product(left, right, precision=lax.Precision.HIGHEST):
    return jnp.dot(left, right, precision=precision, preferred_element_type=jnp.float32)


def local_terms(time_factor, user_block, base_block, count_block, start_block):
    linear = product(time_factor, user_block.T) + base_block[None, :]
    time_bins = jnp.arange(time_factor.shape[0], dtype=jnp.int32)[:, None]
    observed = time_bins >= start_block[None, :]
    decay = jnp.exp(-jnp.abs(linear))
    intensity = jnp.maximum(linear, 0.0) + jnp.log1p(decay) + background
    gate_value = jnp.where(linear >= 0, 1.0, decay) / (1.0 + decay)
    inverse = 1.0 / intensity
    residual = jnp.where(observed, gate_value * (1.0 - count_block.astype(jnp.float32) * inverse), 0.0)
    curvature = jnp.where(observed, gate_value * gate_value * inverse, 0.0)
    return (residual, curvature)


def exchange(value, n, distance):
    return lax.ppermute(value, "user", [(i, i ^ distance) for i in range(n)])


def sum_over_users(partial, n):
    if n == 1:
        return partial, [(partial, 0)]
    if n & (n - 1) or partial.shape[0] % n:
        total = lax.psum(partial, "user")
        return total, [(total, 0)]
    me = lax.axis_index("user")
    distances = []
    d = 1
    while d < n:
        distances.append(d)
        d *= 2
    halving, butterfly = distances[:2], distances[2:]
    block, offset = partial, 0
    for d in halving:
        half = block.shape[0] // 2
        upper = (me // d) % 2
        keep = lax.dynamic_slice_in_dim(block, upper * half, half, 0)
        send = lax.dynamic_slice_in_dim(block, (1 - upper) * half, half, 0)
        offset = offset + upper * half
        block = keep + exchange(send, n, d)
    for d in butterfly:
        block = block + exchange(block, n, d)
    pieces = [(block, offset)]
    for d in reversed(halving):
        rows = block.shape[0]
        other = exchange(block, n, d)
        upper = (me // d) % 2
        pieces.append((other, offset + (1 - 2 * upper) * rows))
        both = jnp.concatenate([block, other], axis=0)
        swapped = jnp.concatenate([other, block], axis=0)
        block = jnp.where(upper == 0, both, swapped)
        offset = offset - upper * rows
    return block, pieces


def sum_scalars(values, n):
    lane = lax.broadcasted_iota(jnp.int32, (n, 1, 128), 2)
    spread = jnp.zeros((n, 1, 128), jnp.float32)
    for k, v in enumerate(values):
        spread = jnp.where(lane == k, v, spread)
    if n > 1:
        spread = lax.all_to_all(spread, "user", 0, 0, tiled=False)
    total = jnp.sum(spread, axis=(0, 1))
    return [total[k] for k in range(len(values))]


def body(n, counts, first_bin, time_factor, user_factor, user_base):
    shard_rows = time_factor.shape[0] // n
    offset = lax.axis_index("user") * shard_rows
    mine_rows = time_factor
    for sweep in range(SWEEPS):
        residual, curvature = local_terms(time_factor, user_factor, user_base, counts, first_bin)
        grad_user = product(residual.T, time_factor)
        grad_whole, pieces = sum_over_users(product(residual, user_factor), n)
        user_norm = jnp.sum(grad_user * grad_user)
        bending = 0.0
        for piece, first in pieces:
            rows = piece.shape[0]
            tangent_image = product(piece, user_factor.T, lax.Precision.HIGH) + product(
                lax.dynamic_slice_in_dim(time_factor, first, rows, 0), grad_user.T, lax.Precision.HIGH
            )
            weight = lax.dynamic_slice_in_dim(curvature, first, rows, 0)
            bending = bending + jnp.sum(weight * tangent_image * tangent_image)
        user_norm_total, bend_total = sum_scalars([user_norm, bending], n)
        norm_total = jnp.sum(grad_whole * grad_whole) + user_norm_total
        relax_step = norm_total / (bend_total + damping * norm_total)
        user_factor = user_factor - relax_step * grad_user
        if sweep + 1 < SWEEPS:
            time_factor = time_factor - relax_step * grad_whole
        else:
            mine_rows = lax.dynamic_slice_in_dim(
                time_factor - relax_step * grad_whole, offset, shard_rows, 0
            )
    return (mine_rows, user_factor)


def solution(mesh):
    n = mesh.shape["user"]
    return jax.shard_map(
        lambda *args: body(n, *args),
        mesh=mesh,
        in_specs=(
            P(None, ("parts", "user")),
            P(("parts", "user")),
            P("parts", None),
            P(("parts", "user"), None),
            P(("parts", "user")),
        ),
        out_specs=(P(("parts", "user"), None), P(("parts", "user"), None)),
        check_vma=False,
    )
```

```python
import jax
import jax.numpy as jnp
from jax import lax
from jax.sharding import PartitionSpec as P

SWEEPS = 2


damping = 0.5
background = 0.5


def product(left, right, precision=lax.Precision.HIGHEST):
    return jnp.dot(left, right, precision=precision, preferred_element_type=jnp.float32)


def local_terms(time_factor, user_block, base_block, count_block, start_block):
    linear = product(time_factor, user_block.T) + base_block[None, :]
    time_bins = jnp.arange(time_factor.shape[0], dtype=jnp.int32)[:, None]
    observed = time_bins >= start_block[None, :]
    decay = jnp.exp(-jnp.abs(linear))
    intensity = jnp.maximum(linear, 0.0) + jnp.log1p(decay) + background
    gate_value = jnp.where(linear >= 0, 1.0, decay) / (1.0 + decay)
    inverse = 1.0 / intensity
    residual = jnp.where(observed, gate_value * (1.0 - count_block.astype(jnp.float32) * inverse), 0.0)
    curvature = jnp.where(observed, gate_value * gate_value * inverse, 0.0)
    return (residual, curvature)


def exchange(value, n, distance):
    return lax.ppermute(value, "user", [(i, i ^ distance) for i in range(n)])


def sum_over_users(partial, n):
    me = lax.axis_index("user")
    if n == 1:
        return partial, [(partial, 0)], jnp.sum(partial * partial)
    if n & (n - 1) or partial.shape[0] % n:
        total = lax.psum(partial, "user")
        return total, [(total, 0)], jnp.where(me == 0, jnp.sum(total * total), 0.0)
    distances = []
    d = 1
    while d < n:
        distances.append(d)
        d *= 2
    halving, butterfly = distances[:2], distances[2:]
    block, offset = partial, 0
    for d in halving:
        half = block.shape[0] // 2
        upper = (me // d) % 2
        keep = lax.dynamic_slice_in_dim(block, upper * half, half, 0)
        send = lax.dynamic_slice_in_dim(block, (1 - upper) * half, half, 0)
        offset = offset + upper * half
        block = keep + exchange(send, n, d)
    for d in butterfly:
        block = block + exchange(block, n, d)
    share = jnp.where(me < 4, jnp.sum(block * block), 0.0)
    pieces = [(block, offset)]
    for d in reversed(halving):
        rows = block.shape[0]
        other = exchange(block, n, d)
        upper = (me // d) % 2
        pieces.append((other, offset + (1 - 2 * upper) * rows))
        both = jnp.concatenate([block, other], axis=0)
        swapped = jnp.concatenate([other, block], axis=0)
        block = jnp.where(upper == 0, both, swapped)
        offset = offset - upper * rows
    return block, pieces, share


def sum_rows(values, n):
    rows = jnp.stack([jnp.broadcast_to(v, (128,)) for v in values])
    spread = jnp.broadcast_to(rows[None], (n,) + rows.shape)
    if n > 1:
        spread = lax.all_to_all(spread, "user", 0, 0, tiled=False)
    total = jnp.sum(spread, axis=0)
    return [total[k:k + 1] for k in range(len(values))]


def body(n, counts, first_bin, time_factor, user_factor, user_base):
    shard_rows = time_factor.shape[0] // n
    offset = lax.axis_index("user") * shard_rows
    mine_rows = time_factor
    for sweep in range(SWEEPS):
        residual, curvature = local_terms(time_factor, user_factor, user_base, counts, first_bin)
        grad_user = product(residual.T, time_factor)
        grad_whole, pieces, time_norm = sum_over_users(product(residual, user_factor), n)
        user_norm = jnp.sum(grad_user * grad_user)
        bending = jnp.zeros((user_factor.shape[0],), jnp.float32)
        for piece, first in pieces:
            rows = piece.shape[0]
            tangent_image = product(piece, user_factor.T, lax.Precision.HIGH) + product(
                lax.dynamic_slice_in_dim(time_factor, first, rows, 0), grad_user.T, lax.Precision.HIGH
            )
            weight = lax.dynamic_slice_in_dim(curvature, first, rows, 0)
            bending = bending + jnp.sum(weight * tangent_image * tangent_image, axis=0)
        norm_total, bend_total = sum_rows([user_norm + time_norm, jnp.sum(bending)], n)
        relax_step = norm_total / (bend_total + damping * norm_total)
        user_factor = user_factor - relax_step * grad_user
        if sweep + 1 < SWEEPS:
            time_factor = time_factor - relax_step * grad_whole
        else:
            mine_rows = lax.dynamic_slice_in_dim(
                time_factor - relax_step * grad_whole, offset, shard_rows, 0
            )
    return (mine_rows, user_factor)


def solution(mesh):
    n = mesh.shape["user"]
    return jax.shard_map(
        lambda *args: body(n, *args),
        mesh=mesh,
        in_specs=(
            P(None, ("parts", "user")),
            P(("parts", "user")),
            P("parts", None),
            P(("parts", "user"), None),
            P(("parts", "user")),
        ),
        out_specs=(P(("parts", "user"), None), P(("parts", "user"), None)),
        check_vma=False,
    )
```

```python
import jax
import jax.numpy as jnp
from jax import lax
from jax.sharding import PartitionSpec as P

SWEEPS = 2


damping = 0.5
background = 0.5


def product(left, right, precision=lax.Precision.HIGHEST):
    return jnp.dot(left, right, precision=precision, preferred_element_type=jnp.float32)


def local_terms(time_factor, user_block, base_block, count_block, start_block):
    linear = product(time_factor, user_block.T) + base_block[None, :]
    time_bins = jnp.arange(time_factor.shape[0], dtype=jnp.int32)[:, None]
    observed = time_bins >= start_block[None, :]
    decay = jnp.exp(-jnp.abs(linear))
    intensity = jnp.maximum(linear, 0.0) + jnp.log1p(decay) + background
    gated = jnp.where(linear >= 0, 1.0, decay) / ((1.0 + decay) * intensity)
    gate_value = gated * intensity
    residual = jnp.where(observed, gate_value - count_block.astype(jnp.float32) * gated, 0.0)
    curvature = jnp.where(observed, gate_value * gated, 0.0)
    return (residual, curvature)


def exchange(value, n, distance):
    return lax.ppermute(value, "user", [(i, i ^ distance) for i in range(n)])


def sum_over_users(partial, n):
    me = lax.axis_index("user")
    if n == 1:
        return partial, [(partial, 0)], jnp.sum(partial * partial)
    if n & (n - 1) or partial.shape[0] % n:
        total = lax.psum(partial, "user")
        return total, [(total, 0)], jnp.where(me == 0, jnp.sum(total * total), 0.0)
    distances = []
    d = 1
    while d < n:
        distances.append(d)
        d *= 2
    halving, butterfly = distances[:2], distances[2:]
    block, offset = partial, 0
    for d in halving:
        half = block.shape[0] // 2
        upper = (me // d) % 2
        keep = lax.dynamic_slice_in_dim(block, upper * half, half, 0)
        send = lax.dynamic_slice_in_dim(block, (1 - upper) * half, half, 0)
        offset = offset + upper * half
        block = keep + exchange(send, n, d)
    for d in butterfly:
        block = block + exchange(block, n, d)
    share = jnp.where(me < 4, jnp.sum(block * block), 0.0)
    pieces = [(block, offset)]
    for d in reversed(halving):
        rows = block.shape[0]
        other = exchange(block, n, d)
        upper = (me // d) % 2
        pieces.append((other, offset + (1 - 2 * upper) * rows))
        both = jnp.concatenate([block, other], axis=0)
        swapped = jnp.concatenate([other, block], axis=0)
        block = jnp.where(upper == 0, both, swapped)
        offset = offset - upper * rows
    return block, pieces, share


def sum_rows(values, n):
    row = lax.broadcasted_iota(jnp.int32, (n, len(values), 128), 1)
    spread = jnp.zeros(row.shape, jnp.float32)
    for k, v in enumerate(values):
        spread = jnp.where(row == k, v, spread)
    if n > 1:
        spread = lax.all_to_all(spread, "user", 0, 0, tiled=False)
    total = jnp.sum(spread, axis=0)
    return [total[k:k + 1] for k in range(len(values))]


def body(n, counts, first_bin, time_factor, user_factor, user_base):
    shard_rows = time_factor.shape[0] // n
    offset = lax.axis_index("user") * shard_rows
    mine_rows = time_factor
    for sweep in range(SWEEPS):
        residual, curvature = local_terms(time_factor, user_factor, user_base, counts, first_bin)
        grad_user = product(residual.T, time_factor)
        grad_whole, pieces, time_norm = sum_over_users(product(residual, user_factor), n)
        user_norm = jnp.sum(grad_user * grad_user)
        bending = jnp.zeros((user_factor.shape[0],), jnp.float32)
        for piece, first in pieces:
            rows = piece.shape[0]
            tangent_image = product(piece, user_factor.T, lax.Precision.HIGH) + product(
                lax.dynamic_slice_in_dim(time_factor, first, rows, 0), grad_user.T, lax.Precision.HIGH
            )
            weight = lax.dynamic_slice_in_dim(curvature, first, rows, 0)
            bending = bending + jnp.sum(weight * tangent_image * tangent_image, axis=0)
        norm_total, bend_total = sum_rows([user_norm + time_norm, jnp.sum(bending)], n)
        relax_step = norm_total / (bend_total + damping * norm_total)
        user_factor = user_factor - relax_step * grad_user
        if sweep + 1 < SWEEPS:
            time_factor = time_factor - relax_step * grad_whole
        else:
            mine_rows = lax.dynamic_slice_in_dim(
                time_factor - relax_step * grad_whole, offset, shard_rows, 0
            )
    return (mine_rows, user_factor)


def solution(mesh):
    n = mesh.shape["user"]
    return jax.shard_map(
        lambda *args: body(n, *args),
        mesh=mesh,
        in_specs=(
            P(None, ("parts", "user")),
            P(("parts", "user")),
            P("parts", None),
            P(("parts", "user"), None),
            P(("parts", "user")),
        ),
        out_specs=(P(("parts", "user"), None), P(("parts", "user"), None)),
        check_vma=False,
    )
```

```python
import jax
import jax.numpy as jnp
from jax import lax
from jax.sharding import PartitionSpec as P

SWEEPS = 2


damping = 0.5
background = 0.5


def product(left, right, precision=lax.Precision.HIGHEST):
    return jnp.dot(left, right, precision=precision, preferred_element_type=jnp.float32)


def local_terms(time_factor, user_block, base_block, count_block, start_block, first_bin=0):
    linear = product(time_factor, user_block.T) + base_block[None, :]
    time_bins = first_bin + jnp.arange(time_factor.shape[0], dtype=jnp.int32)[:, None]
    observed = time_bins >= start_block[None, :]
    decay = jnp.exp(-jnp.abs(linear))
    intensity = jnp.maximum(linear, 0.0) + jnp.log1p(decay) + background
    gated = jnp.where(linear >= 0, 1.0, decay) / ((1.0 + decay) * intensity)
    gate_value = gated * intensity
    residual = jnp.where(observed, gate_value - count_block.astype(jnp.float32) * gated, 0.0)
    curvature = jnp.where(observed, gate_value * gated, 0.0)
    return (residual, curvature)


def exchange(value, n, distance):
    return lax.ppermute(value, "user", [(i, i ^ distance) for i in range(n)])


def distances_of(n):
    distances = []
    d = 1
    while d < n:
        distances.append(d)
        d *= 2
    return distances


def finish_sum(block, offset, n, halving, butterfly):
    me = lax.axis_index("user")
    for d in halving[1:]:
        half = block.shape[0] // 2
        upper = (me // d) % 2
        keep = lax.dynamic_slice_in_dim(block, upper * half, half, 0)
        send = lax.dynamic_slice_in_dim(block, (1 - upper) * half, half, 0)
        offset = offset + upper * half
        block = keep + exchange(send, n, d)
    for d in butterfly:
        block = block + exchange(block, n, d)
    share = jnp.where(me < 2 ** len(halving), jnp.sum(block * block), 0.0)
    pieces = [(block, offset)]
    for d in reversed(halving[1:]):
        rows = block.shape[0]
        other = exchange(block, n, d)
        upper = (me // d) % 2
        pieces.append((other, offset + (1 - 2 * upper) * rows))
        both = jnp.concatenate([block, other], axis=0)
        swapped = jnp.concatenate([other, block], axis=0)
        block = jnp.where(upper == 0, both, swapped)
        offset = offset - upper * rows
    return block, pieces, share


def sum_rows(values, n):
    row = lax.broadcasted_iota(jnp.int32, (n, len(values), 128), 1)
    spread = jnp.zeros(row.shape, jnp.float32)
    for k, v in enumerate(values):
        spread = jnp.where(row == k, v, spread)
    if n > 1:
        spread = lax.all_to_all(spread, "user", 0, 0, tiled=False)
    total = jnp.sum(spread, axis=0)
    return [total[k:k + 1] for k in range(len(values))]


def bending_of(pieces, time_factor, user_factor, grad_user):
    bending = jnp.zeros((user_factor.shape[0],), jnp.float32)
    for piece, first, weight in pieces:
        rows = piece.shape[0]
        tangent_image = product(piece, user_factor.T, lax.Precision.HIGH) + product(
            lax.dynamic_slice_in_dim(time_factor, first, rows, 0), grad_user.T, lax.Precision.HIGH
        )
        bending = bending + jnp.sum(weight * tangent_image * tangent_image, axis=0)
    return jnp.sum(bending)


def gradients_split(n, counts, first_bin, time_factor, user_factor, user_base):
    me = lax.axis_index("user")
    distances = distances_of(n)
    halving, butterfly = distances[:2], distances[2:]
    half = time_factor.shape[0] // 2
    upper = me % 2
    sent_first, kept_first = (1 - upper) * half, upper * half

    def terms(first):
        rows = lax.dynamic_slice_in_dim(time_factor, first, half, 0)
        block = lax.dynamic_slice_in_dim(counts, first, half, 0)
        residual, curvature = local_terms(rows, user_factor, user_base, block, first_bin, first)
        return rows, residual, curvature

    sent_rows, sent_residual, sent_curvature = terms(sent_first)
    arrived = exchange(product(sent_residual, user_factor), n, 1)
    kept_rows, kept_residual, kept_curvature = terms(kept_first)
    grad_user = product(sent_residual.T, sent_rows) + product(kept_residual.T, kept_rows)
    kept, pieces, time_norm = finish_sum(
        product(kept_residual, user_factor) + arrived, kept_first, n, halving, butterfly
    )
    other = exchange(kept, n, 1)
    grad_whole = jnp.where(upper == 0, jnp.concatenate([kept, other]), jnp.concatenate([other, kept]))
    weighted = [
        (piece, first, lax.dynamic_slice_in_dim(kept_curvature, first - kept_first, piece.shape[0], 0))
        for piece, first in pieces
    ]
    weighted.append((other, sent_first, sent_curvature))
    return grad_user, grad_whole, time_norm, bending_of(weighted, time_factor, user_factor, grad_user)


def gradients_whole(n, counts, first_bin, time_factor, user_factor, user_base):
    me = lax.axis_index("user")
    residual, curvature = local_terms(time_factor, user_factor, user_base, counts, first_bin)
    grad_user = product(residual.T, time_factor)
    grad_whole = lax.psum(product(residual, user_factor), "user") if n > 1 else product(residual, user_factor)
    time_norm = jnp.where(me == 0, jnp.sum(grad_whole * grad_whole), 0.0)
    bending = bending_of([(grad_whole, 0, curvature)], time_factor, user_factor, grad_user)
    return grad_user, grad_whole, time_norm, bending


def body(n, counts, first_bin, time_factor, user_factor, user_base):
    shard_rows = time_factor.shape[0] // n
    offset = lax.axis_index("user") * shard_rows
    split = n >= 4 and not n & (n - 1) and time_factor.shape[0] % n == 0
    gradients = gradients_split if split else gradients_whole
    mine_rows = time_factor
    for sweep in range(SWEEPS):
        grad_user, grad_whole, time_norm, bending = gradients(
            n, counts, first_bin, time_factor, user_factor, user_base
        )
        user_norm = jnp.sum(grad_user * grad_user)
        norm_total, bend_total = sum_rows([user_norm + time_norm, bending], n)
        relax_step = norm_total / (bend_total + damping * norm_total)
        user_factor = user_factor - relax_step * grad_user
        if sweep + 1 < SWEEPS:
            time_factor = time_factor - relax_step * grad_whole
        else:
            mine_rows = lax.dynamic_slice_in_dim(
                time_factor - relax_step * grad_whole, offset, shard_rows, 0
            )
    return (mine_rows, user_factor)


def solution(mesh):
    n = mesh.shape["user"]
    return jax.shard_map(
        lambda *args: body(n, *args),
        mesh=mesh,
        in_specs=(
            P(None, ("parts", "user")),
            P(("parts", "user")),
            P("parts", None),
            P(("parts", "user"), None),
            P(("parts", "user")),
        ),
        out_specs=(P(("parts", "user"), None), P(("parts", "user"), None)),
        check_vma=False,
    )
```

```python
import jax
import jax.numpy as jnp
from jax import lax
from jax.sharding import PartitionSpec as P

SWEEPS = 2


damping = 0.5
background = 0.5


def product(left, right, precision=lax.Precision.HIGHEST):
    return jnp.dot(left, right, precision=precision, preferred_element_type=jnp.float32)


def local_terms(time_factor, user_block, base_block, count_block, observed):
    linear = product(time_factor, user_block.T) + base_block[None, :]
    decay = jnp.exp(-jnp.abs(linear))
    intensity = jnp.maximum(linear, 0.0) + jnp.log1p(decay) + background
    gate_value = jnp.where(linear >= 0, 1.0, decay) / (1.0 + decay)
    inverse = 1.0 / intensity
    residual = jnp.where(observed, gate_value * (1.0 - count_block.astype(jnp.float32) * inverse), 0.0)
    curvature = jnp.where(observed, gate_value * gate_value * inverse, 0.0)
    return (residual, curvature)


def observed_of(counts, first_bin):
    time_bins = jnp.arange(counts.shape[0], dtype=jnp.int32)[:, None]
    return time_bins >= first_bin[None, :]


def exchange(value, n, distance):
    return lax.ppermute(value, "user", [(i, i ^ distance) for i in range(n)])


def sum_over_users(partial, n):
    me = lax.axis_index("user")
    if n == 1:
        return partial, [(partial, 0)], jnp.sum(partial * partial)
    if n & (n - 1) or partial.shape[0] % n:
        total = lax.psum(partial, "user")
        return total, [(total, 0)], jnp.where(me == 0, jnp.sum(total * total), 0.0)
    distances = []
    d = 1
    while d < n:
        distances.append(d)
        d *= 2
    halving, butterfly = distances[:2], distances[2:]
    block, offset = partial, 0
    for d in halving:
        half = block.shape[0] // 2
        upper = (me // d) % 2
        keep = lax.dynamic_slice_in_dim(block, upper * half, half, 0)
        send = lax.dynamic_slice_in_dim(block, (1 - upper) * half, half, 0)
        offset = offset + upper * half
        block = keep + exchange(send, n, d)
    for d in butterfly:
        block = block + exchange(block, n, d)
    share = jnp.where(me < 4, jnp.sum(block * block), 0.0)
    pieces = [(block, offset)]
    for d in reversed(halving):
        rows = block.shape[0]
        other = exchange(block, n, d)
        upper = (me // d) % 2
        pieces.append((other, offset + (1 - 2 * upper) * rows))
        both = jnp.concatenate([block, other], axis=0)
        swapped = jnp.concatenate([other, block], axis=0)
        block = jnp.where(upper == 0, both, swapped)
        offset = offset - upper * rows
    return block, pieces, share


def sum_rows(values, n):
    rows = jnp.stack([jnp.broadcast_to(v, (128,)) for v in values])
    spread = jnp.broadcast_to(rows[None], (n,) + rows.shape)
    if n > 1:
        spread = lax.all_to_all(spread, "user", 0, 0, tiled=False)
    total = jnp.sum(spread, axis=0)
    return [total[k:k + 1] for k in range(len(values))]


def body(n, counts, first_bin, time_factor, user_factor, user_base):
    shard_rows = time_factor.shape[0] // n
    offset = lax.axis_index("user") * shard_rows
    mine_rows = time_factor
    observed = observed_of(counts, first_bin)
    for sweep in range(SWEEPS):
        residual, curvature = local_terms(time_factor, user_factor, user_base, counts, observed)
        if sweep + 1 < SWEEPS:
            code = lax.optimization_barrier(jnp.where(observed, counts, -1).astype(jnp.int8))
        grad_user = product(residual.T, time_factor)
        grad_whole, pieces, time_norm = sum_over_users(product(residual, user_factor), n)
        user_norm = jnp.sum(grad_user * grad_user)
        bending = jnp.zeros((user_factor.shape[0],), jnp.float32)
        for piece, first in pieces:
            rows = piece.shape[0]
            tangent_image = product(piece, user_factor.T, lax.Precision.HIGH) + product(
                lax.dynamic_slice_in_dim(time_factor, first, rows, 0), grad_user.T, lax.Precision.HIGH
            )
            weight = lax.dynamic_slice_in_dim(curvature, first, rows, 0)
            bending = bending + jnp.sum(weight * tangent_image * tangent_image, axis=0)
        norm_total, bend_total = sum_rows([user_norm + time_norm, jnp.sum(bending)], n)
        relax_step = norm_total / (bend_total + damping * norm_total)
        user_factor = user_factor - relax_step * grad_user
        if sweep + 1 < SWEEPS:
            time_factor = time_factor - relax_step * grad_whole
            counts, observed = code, code >= 0
        else:
            mine_rows = lax.dynamic_slice_in_dim(
                time_factor - relax_step * grad_whole, offset, shard_rows, 0
            )
    return (mine_rows, user_factor)


def solution(mesh):
    n = mesh.shape["user"]
    return jax.shard_map(
        lambda *args: body(n, *args),
        mesh=mesh,
        in_specs=(
            P(None, ("parts", "user")),
            P(("parts", "user")),
            P("parts", None),
            P(("parts", "user"), None),
            P(("parts", "user")),
        ),
        out_specs=(P(("parts", "user"), None), P(("parts", "user"), None)),
        check_vma=False,
    )
```

```python
import jax
import jax.numpy as jnp
from jax import lax
from jax.sharding import PartitionSpec as P

SWEEPS = 2


damping = 0.5
background = 0.5


def product(left, right, precision=lax.Precision.HIGH):
    return jnp.dot(left, right, precision=precision, preferred_element_type=jnp.float32)


def local_terms(time_factor, user_block, base_block, count_block, start_block):
    linear = product(time_factor, user_block.T) + base_block[None, :]
    time_bins = jnp.arange(time_factor.shape[0], dtype=jnp.int32)[:, None]
    observed = time_bins >= start_block[None, :]
    decay = jnp.exp(-jnp.abs(linear))
    intensity = jnp.maximum(linear, 0.0) + jnp.log1p(decay) + background
    gate_value = jnp.where(linear >= 0, 1.0, decay) / (1.0 + decay)
    inverse = 1.0 / intensity
    residual = jnp.where(observed, gate_value * (1.0 - count_block.astype(jnp.float32) * inverse), 0.0)
    curvature = jnp.where(observed, gate_value * gate_value * inverse, 0.0)
    return (residual, curvature)


def exchange(value, n, distance):
    return lax.ppermute(value, "user", [(i, i ^ distance) for i in range(n)])


def sum_over_users(partial, n):
    me = lax.axis_index("user")
    if n == 1:
        return partial, [(partial, 0)], jnp.sum(partial * partial)
    if n & (n - 1) or partial.shape[0] % n:
        total = lax.psum(partial, "user")
        return total, [(total, 0)], jnp.where(me == 0, jnp.sum(total * total), 0.0)
    distances = []
    d = 1
    while d < n:
        distances.append(d)
        d *= 2
    halving, butterfly = distances[:2], distances[2:]
    block, offset = partial, 0
    for d in halving:
        half = block.shape[0] // 2
        upper = (me // d) % 2
        keep = lax.dynamic_slice_in_dim(block, upper * half, half, 0)
        send = lax.dynamic_slice_in_dim(block, (1 - upper) * half, half, 0)
        offset = offset + upper * half
        block = keep + exchange(send, n, d)
    for d in butterfly:
        block = block + exchange(block, n, d)
    share = jnp.where(me < 4, jnp.sum(block * block), 0.0)
    pieces = [(block, offset)]
    for d in reversed(halving):
        rows = block.shape[0]
        other = exchange(block, n, d)
        upper = (me // d) % 2
        pieces.append((other, offset + (1 - 2 * upper) * rows))
        both = jnp.concatenate([block, other], axis=0)
        swapped = jnp.concatenate([other, block], axis=0)
        block = jnp.where(upper == 0, both, swapped)
        offset = offset - upper * rows
    return block, pieces, share


def sum_rows(values, n):
    rows = jnp.stack([jnp.broadcast_to(v, (128,)) for v in values])
    spread = jnp.broadcast_to(rows[None], (n,) + rows.shape)
    if n > 1:
        spread = lax.all_to_all(spread, "user", 0, 0, tiled=False)
    total = jnp.sum(spread, axis=0)
    return [total[k:k + 1] for k in range(len(values))]


def body(n, counts, first_bin, time_factor, user_factor, user_base):
    shard_rows = time_factor.shape[0] // n
    offset = lax.axis_index("user") * shard_rows
    mine_rows = time_factor
    for sweep in range(SWEEPS):
        residual, curvature = local_terms(time_factor, user_factor, user_base, counts, first_bin)
        grad_user = product(residual.T, time_factor)
        grad_whole, pieces, time_norm = sum_over_users(product(residual, user_factor), n)
        user_norm = jnp.sum(grad_user * grad_user)
        bending = jnp.zeros((user_factor.shape[0],), jnp.float32)
        for piece, first in pieces:
            rows = piece.shape[0]
            tangent_image = product(piece, user_factor.T) + product(
                lax.dynamic_slice_in_dim(time_factor, first, rows, 0), grad_user.T
            )
            weight = lax.dynamic_slice_in_dim(curvature, first, rows, 0)
            bending = bending + jnp.sum(weight * tangent_image * tangent_image, axis=0)
        norm_total, bend_total = sum_rows([user_norm + time_norm, jnp.sum(bending)], n)
        relax_step = norm_total / (bend_total + damping * norm_total)
        user_factor = user_factor - relax_step * grad_user
        if sweep + 1 < SWEEPS:
            time_factor = time_factor - relax_step * grad_whole
        else:
            mine_rows = lax.dynamic_slice_in_dim(
                time_factor - relax_step * grad_whole, offset, shard_rows, 0
            )
    return (mine_rows, user_factor)


def solution(mesh):
    n = mesh.shape["user"]
    return jax.shard_map(
        lambda *args: body(n, *args),
        mesh=mesh,
        in_specs=(
            P(None, ("parts", "user")),
            P(("parts", "user")),
            P("parts", None),
            P(("parts", "user"), None),
            P(("parts", "user")),
        ),
        out_specs=(P(("parts", "user"), None), P(("parts", "user"), None)),
        check_vma=False,
    )
```

```python
import jax
import jax.numpy as jnp
from jax import lax
from jax.sharding import PartitionSpec as P

SWEEPS = 2


damping = 0.5
background = 0.5


def product(left, right, precision=lax.Precision.HIGH):
    return jnp.dot(left, right, precision=precision, preferred_element_type=jnp.float32)


def local_terms(time_factor, user_block, base_block, count_block, start_block):
    linear = product(time_factor, user_block.T) + base_block[None, :]
    time_bins = jnp.arange(time_factor.shape[0], dtype=jnp.int32)[:, None]
    observed = time_bins >= start_block[None, :]
    decay = jnp.exp(-jnp.abs(linear))
    intensity = jnp.maximum(linear, 0.0) + jnp.log1p(decay) + background
    gate_value = jnp.where(linear >= 0, 1.0, decay) / (1.0 + decay)
    inverse = 1.0 / intensity
    residual = jnp.where(observed, gate_value * (1.0 - count_block.astype(jnp.float32) * inverse), 0.0)
    curvature = jnp.where(observed, gate_value * gate_value * inverse, 0.0)
    return (residual, curvature)


def exchange(value, n, distance):
    return lax.ppermute(value, "user", [(i, i ^ distance) for i in range(n)])


def sum_over_users(partial, n):
    me = lax.axis_index("user")
    if n == 1:
        return partial, [(partial, 0)], jnp.sum(partial * partial)
    if n & (n - 1) or partial.shape[0] % n:
        total = lax.psum(partial, "user")
        return total, [(total, 0)], jnp.where(me == 0, jnp.sum(total * total), 0.0)
    distances = []
    d = 1
    while d < n:
        distances.append(d)
        d *= 2
    halving, butterfly = distances[:2], distances[2:]
    block, offset = partial, 0
    for d in halving:
        half = block.shape[0] // 2
        upper = (me // d) % 2
        keep = lax.dynamic_slice_in_dim(block, upper * half, half, 0)
        send = lax.dynamic_slice_in_dim(block, (1 - upper) * half, half, 0)
        offset = offset + upper * half
        block = keep + exchange(send, n, d)
    for d in butterfly:
        block = block + exchange(block, n, d)
    share = jnp.where(me < 4, jnp.sum(block * block), 0.0)
    pieces = [(block, offset)]
    for level in reversed(range(len(halving))):
        d = halving[level]
        shift = (1 - 2 * ((me // d) % 2)) * (partial.shape[0] >> (level + 1))
        pieces = pieces + [(exchange(piece, n, d), first + shift) for piece, first in pieces]
    block = jnp.zeros_like(partial)
    for piece, first in pieces:
        block = lax.dynamic_update_slice_in_dim(block, piece, first, 0)
    return block, pieces, share


def sum_rows(values, n):
    rows = jnp.stack([jnp.broadcast_to(v, (128,)) for v in values])
    spread = jnp.broadcast_to(rows[None], (n,) + rows.shape)
    if n > 1:
        spread = lax.all_to_all(spread, "user", 0, 0, tiled=False)
    total = jnp.sum(spread, axis=0)
    return [total[k:k + 1] for k in range(len(values))]


def body(n, counts, first_bin, time_factor, user_factor, user_base):
    shard_rows = time_factor.shape[0] // n
    offset = lax.axis_index("user") * shard_rows
    mine_rows = time_factor
    for sweep in range(SWEEPS):
        residual, curvature = local_terms(time_factor, user_factor, user_base, counts, first_bin)
        grad_user = product(residual.T, time_factor)
        grad_whole, pieces, time_norm = sum_over_users(product(residual, user_factor), n)
        user_norm = jnp.sum(grad_user * grad_user)
        bending = jnp.zeros((user_factor.shape[0],), jnp.float32)
        for piece, first in pieces:
            rows = piece.shape[0]
            tangent_image = product(piece, user_factor.T) + product(
                lax.dynamic_slice_in_dim(time_factor, first, rows, 0), grad_user.T
            )
            weight = lax.dynamic_slice_in_dim(curvature, first, rows, 0)
            bending = bending + jnp.sum(weight * tangent_image * tangent_image, axis=0)
        norm_total, bend_total = sum_rows([user_norm + time_norm, jnp.sum(bending)], n)
        relax_step = norm_total / (bend_total + damping * norm_total)
        user_factor = user_factor - relax_step * grad_user
        if sweep + 1 < SWEEPS:
            time_factor = time_factor - relax_step * grad_whole
        else:
            mine_rows = lax.dynamic_slice_in_dim(
                time_factor - relax_step * grad_whole, offset, shard_rows, 0
            )
    return (mine_rows, user_factor)


def solution(mesh):
    n = mesh.shape["user"]
    return jax.shard_map(
        lambda *args: body(n, *args),
        mesh=mesh,
        in_specs=(
            P(None, ("parts", "user")),
            P(("parts", "user")),
            P("parts", None),
            P(("parts", "user"), None),
            P(("parts", "user")),
        ),
        out_specs=(P(("parts", "user"), None), P(("parts", "user"), None)),
        check_vma=False,
    )
```

```python
import jax
import jax.numpy as jnp
from jax import lax
from jax.sharding import PartitionSpec as P

SWEEPS = 2


damping = 0.5
background = 0.5


def product(left, right, precision=lax.Precision.HIGH):
    return jnp.dot(left, right, precision=precision, preferred_element_type=jnp.float32)


def local_terms(time_factor, user_block, base_block, count_block, start_block):
    linear = product(time_factor, user_block.T) + base_block[None, :]
    time_bins = jnp.arange(time_factor.shape[0], dtype=jnp.int32)[:, None]
    observed = time_bins >= start_block[None, :]
    decay = jnp.exp(-jnp.abs(linear))
    intensity = jnp.maximum(linear, 0.0) + jnp.log1p(decay) + background
    gate_value = jnp.where(linear >= 0, 1.0, decay) / (1.0 + decay)
    inverse = 1.0 / intensity
    residual = jnp.where(observed, gate_value * (1.0 - count_block.astype(jnp.float32) * inverse), 0.0)
    curvature = jnp.where(observed, gate_value * gate_value * inverse, 0.0)
    return (residual, curvature)


def exchange(value, n, distance):
    return lax.ppermute(value, "user", [(i, i ^ distance) for i in range(n)])


def sum_over_users(partial, n):
    me = lax.axis_index("user")
    if n == 1:
        return partial, [(partial, 0)], jnp.sum(partial * partial)
    if n & (n - 1) or partial.shape[0] % n:
        total = lax.psum(partial, "user")
        return total, [(total, 0)], jnp.where(me == 0, jnp.sum(total * total), 0.0)
    distances = []
    d = 1
    while d < n:
        distances.append(d)
        d *= 2
    halving, butterfly = distances[:2], distances[2:]
    block, offset = partial, 0
    for d in halving:
        half = block.shape[0] // 2
        upper = (me // d) % 2
        keep = lax.dynamic_slice_in_dim(block, upper * half, half, 0)
        send = lax.dynamic_slice_in_dim(block, (1 - upper) * half, half, 0)
        offset = offset + upper * half
        block = keep + exchange(send, n, d)
    for d in butterfly:
        block = block + exchange(block, n, d)
    share = jnp.where(me < 4, jnp.sum(block * block), 0.0)
    pieces = [(block, offset)]
    for level in reversed(range(len(halving))):
        d = halving[level]
        shift = (1 - 2 * ((me // d) % 2)) * (partial.shape[0] >> (level + 1))
        pieces = pieces + [(exchange(piece, n, d), first + shift) for piece, first in pieces]
    block = jnp.zeros_like(partial)
    for piece, first in pieces:
        block = lax.dynamic_update_slice_in_dim(block, piece, first, 0)
    return block, pieces, share


def sum_rows(values, n):
    rows = jnp.stack([jnp.broadcast_to(v, (128,)) for v in values])
    spread = jnp.broadcast_to(rows[None], (n,) + rows.shape)
    if n > 1:
        spread = lax.all_to_all(spread, "user", 0, 0, tiled=False)
    total = jnp.sum(spread, axis=0)
    return [total[k:k + 1] for k in range(len(values))]


def body(n, counts, first_bin, time_factor, user_factor, user_base):
    shard_rows = time_factor.shape[0] // n
    offset = lax.axis_index("user") * shard_rows
    mine_rows = time_factor
    for sweep in range(SWEEPS):
        residual, curvature = local_terms(time_factor, user_factor, user_base, counts, first_bin)
        grad_user = product(residual.T, time_factor)
        grad_whole, pieces, time_norm = sum_over_users(product(residual, user_factor), n)
        user_norm = jnp.sum(grad_user * grad_user)
        bending = jnp.zeros((user_factor.shape[0],), jnp.float32)
        for piece, first in pieces:
            rows = piece.shape[0]
            tangent_image = product(piece, user_factor.T) + product(
                lax.dynamic_slice_in_dim(time_factor, first, rows, 0), grad_user.T
            )
            weight = lax.dynamic_slice_in_dim(curvature, first, rows, 0)
            bending = bending + jnp.sum(weight * tangent_image * tangent_image, axis=0)
        if sweep + 1 == SWEEPS:
            mine_time, mine_grad = lax.optimization_barrier((
                lax.dynamic_slice_in_dim(time_factor, offset, shard_rows, 0),
                lax.dynamic_slice_in_dim(grad_whole, offset, shard_rows, 0),
            ))
        norm_total, bend_total = sum_rows([user_norm + time_norm, jnp.sum(bending)], n)
        relax_step = norm_total / (bend_total + damping * norm_total)
        user_factor = user_factor - relax_step * grad_user
        if sweep + 1 < SWEEPS:
            time_factor = time_factor - relax_step * grad_whole
        else:
            mine_rows = mine_time - relax_step * mine_grad
    return (mine_rows, user_factor)


def solution(mesh):
    n = mesh.shape["user"]
    return jax.shard_map(
        lambda *args: body(n, *args),
        mesh=mesh,
        in_specs=(
            P(None, ("parts", "user")),
            P(("parts", "user")),
            P("parts", None),
            P(("parts", "user"), None),
            P(("parts", "user")),
        ),
        out_specs=(P(("parts", "user"), None), P(("parts", "user"), None)),
        check_vma=False,
    )
```

```python
import jax
import jax.numpy as jnp
from jax import lax
from jax.sharding import PartitionSpec as P

SWEEPS = 2


damping = 0.5
background = 0.5


def product(left, right, precision=lax.Precision.HIGH):
    return jnp.dot(left, right, precision=precision, preferred_element_type=jnp.float32)


def local_terms(time_factor, user_block, base_block, count_block, start_block):
    linear = product(time_factor, user_block.T) + base_block[None, :]
    time_bins = jnp.arange(time_factor.shape[0], dtype=jnp.int32)[:, None]
    observed = time_bins >= start_block[None, :]
    decay = jnp.exp(-jnp.abs(linear))
    intensity = jnp.maximum(linear, 0.0) + jnp.log1p(decay) + background
    gate_value = jnp.where(linear >= 0, 1.0, decay) / (1.0 + decay)
    inverse = 1.0 / intensity
    residual = jnp.where(observed, gate_value * (1.0 - count_block.astype(jnp.float32) * inverse), 0.0)
    curvature = jnp.where(observed, gate_value * gate_value * inverse, 0.0)
    return (residual, curvature)


def exchange(value, n, distance):
    return lax.ppermute(value, "user", [(i, i ^ distance) for i in range(n)])


def sum_over_users(partial, n):
    me = lax.axis_index("user")
    if n == 1:
        return partial, [(partial, 0)], jnp.sum(partial * partial)
    if n & (n - 1) or partial.shape[0] % n:
        total = lax.psum(partial, "user")
        return total, [(total, 0)], jnp.where(me == 0, jnp.sum(total * total), 0.0)
    distances = []
    d = 1
    while d < n:
        distances.append(d)
        d *= 2
    halving, butterfly = distances[:2], distances[2:]
    block, offset = partial, 0
    for d in halving:
        half = block.shape[0] // 2
        upper = (me // d) % 2
        keep = lax.dynamic_slice_in_dim(block, upper * half, half, 0)
        send = lax.dynamic_slice_in_dim(block, (1 - upper) * half, half, 0)
        offset = offset + upper * half
        block = keep + exchange(send, n, d)
    for d in butterfly:
        block = block + exchange(block, n, d)
    share = jnp.where(me < 4, jnp.sum(block * block), 0.0)
    def first_row(j):
        return sum(((j // d) % 2) * (partial.shape[0] >> (level + 1)) for level, d in enumerate(halving))

    pieces = [(block, offset)] + [
        (exchange(block, n, x), first_row(me ^ x)) for x in range(1, 2 ** len(halving))
    ]
    block = jnp.zeros_like(partial)
    for piece, first in pieces:
        block = lax.dynamic_update_slice_in_dim(block, piece, first, 0)
    return block, pieces, share


def sum_rows(values, n):
    rows = jnp.stack([jnp.broadcast_to(v, (128,)) for v in values])
    spread = jnp.broadcast_to(rows[None], (n,) + rows.shape)
    if n > 1:
        spread = lax.all_to_all(spread, "user", 0, 0, tiled=False)
    total = jnp.sum(spread, axis=0)
    return [total[k:k + 1] for k in range(len(values))]


def body(n, counts, first_bin, time_factor, user_factor, user_base):
    shard_rows = time_factor.shape[0] // n
    offset = lax.axis_index("user") * shard_rows
    mine_rows = time_factor
    for sweep in range(SWEEPS):
        residual, curvature = local_terms(time_factor, user_factor, user_base, counts, first_bin)
        grad_user = product(residual.T, time_factor)
        grad_whole, pieces, time_norm = sum_over_users(product(residual, user_factor), n)
        user_norm = jnp.sum(grad_user * grad_user)
        bending = jnp.zeros((user_factor.shape[0],), jnp.float32)
        for piece, first in pieces:
            rows = piece.shape[0]
            tangent_image = product(piece, user_factor.T) + product(
                lax.dynamic_slice_in_dim(time_factor, first, rows, 0), grad_user.T
            )
            weight = lax.dynamic_slice_in_dim(curvature, first, rows, 0)
            bending = bending + jnp.sum(weight * tangent_image * tangent_image, axis=0)
        norm_total, bend_total = sum_rows([user_norm + time_norm, jnp.sum(bending)], n)
        relax_step = norm_total / (bend_total + damping * norm_total)
        user_factor = user_factor - relax_step * grad_user
        if sweep + 1 < SWEEPS:
            time_factor = time_factor - relax_step * grad_whole
        else:
            mine_rows = lax.dynamic_slice_in_dim(
                time_factor - relax_step * grad_whole, offset, shard_rows, 0
            )
    return (mine_rows, user_factor)


def solution(mesh):
    n = mesh.shape["user"]
    return jax.shard_map(
        lambda *args: body(n, *args),
        mesh=mesh,
        in_specs=(
            P(None, ("parts", "user")),
            P(("parts", "user")),
            P("parts", None),
            P(("parts", "user"), None),
            P(("parts", "user")),
        ),
        out_specs=(P(("parts", "user"), None), P(("parts", "user"), None)),
        check_vma=False,
    )
```

```python
import jax
import jax.numpy as jnp
from jax import lax
from jax.sharding import PartitionSpec as P

SWEEPS = 2


damping = 0.5
background = 0.5


def product(left, right, precision=lax.Precision.HIGH):
    return jnp.dot(left, right, precision=precision, preferred_element_type=jnp.float32)


def local_terms(time_factor, user_block, base_block, count_block, start_block):
    linear = product(time_factor, user_block.T) + base_block[None, :]
    time_bins = jnp.arange(time_factor.shape[0], dtype=jnp.int32)[:, None]
    observed = time_bins >= start_block[None, :]
    decay = jnp.exp(-jnp.abs(linear))
    intensity = jnp.maximum(linear, 0.0) + jnp.log1p(decay) + background
    gate_value = jnp.where(linear >= 0, 1.0, decay) / (1.0 + decay)
    inverse = 1.0 / intensity
    residual = jnp.where(observed, gate_value * (1.0 - count_block.astype(jnp.float32) * inverse), 0.0)
    curvature = jnp.where(observed, gate_value * gate_value * inverse, 0.0)
    return (residual, curvature)


def exchange(value, n, distance):
    return lax.ppermute(value, "user", [(i, i ^ distance) for i in range(n)])


def sum_over_users(partial, n):
    me = lax.axis_index("user")
    if n == 1:
        return partial, [(partial, 0)], jnp.sum(partial * partial)
    if n & (n - 1) or partial.shape[0] % n:
        total = lax.psum(partial, "user")
        return total, [(total, 0)], jnp.where(me == 0, jnp.sum(total * total), 0.0)
    distances = []
    d = 1
    while d < n:
        distances.append(d)
        d *= 2
    halving, butterfly = distances[:2], distances[2:]
    block, offset = partial, 0
    for d in halving:
        half = block.shape[0] // 2
        upper = (me // d) % 2
        keep = lax.dynamic_slice_in_dim(block, upper * half, half, 0)
        send = lax.dynamic_slice_in_dim(block, (1 - upper) * half, half, 0)
        offset = offset + upper * half
        block = keep + exchange(send, n, d)
    for d in butterfly:
        block = block + exchange(block, n, d)
    share = jnp.where(me < 4, jnp.sum(block * block), 0.0)
    pieces = [(block, offset)]
    for level in reversed(range(len(halving))):
        d = halving[level]
        shift = (1 - 2 * ((me // d) % 2)) * (partial.shape[0] >> (level + 1))
        pieces = pieces + [(exchange(piece, n, d), first + shift) for piece, first in pieces]
    block = jnp.zeros_like(partial)
    for piece, first in pieces:
        block = lax.dynamic_update_slice_in_dim(block, piece, first, 0)
    return block, pieces, share


def sum_rows(values, n):
    row = lax.broadcasted_iota(jnp.int32, (n, len(values), 128), 1)
    spread = jnp.zeros(row.shape, jnp.float32)
    for k, v in enumerate(values):
        spread = jnp.where(row == k, v, spread)
    if n > 1:
        spread = lax.all_to_all(spread, "user", 0, 0, tiled=False)
    total = jnp.sum(spread, axis=0)
    return [total[k:k + 1] for k in range(len(values))]


def body(n, counts, first_bin, time_factor, user_factor, user_base):
    shard_rows = time_factor.shape[0] // n
    offset = lax.axis_index("user") * shard_rows
    mine_rows = time_factor
    for sweep in range(SWEEPS):
        residual, curvature = local_terms(time_factor, user_factor, user_base, counts, first_bin)
        grad_user = product(residual.T, time_factor)
        grad_whole, pieces, time_norm = sum_over_users(product(residual, user_factor), n)
        user_norm = jnp.sum(grad_user * grad_user)
        bending = jnp.zeros((user_factor.shape[0],), jnp.float32)
        for piece, first in pieces:
            rows = piece.shape[0]
            tangent_image = product(piece, user_factor.T) + product(
                lax.dynamic_slice_in_dim(time_factor, first, rows, 0), grad_user.T
            )
            weight = lax.dynamic_slice_in_dim(curvature, first, rows, 0)
            bending = bending + jnp.sum(weight * tangent_image * tangent_image, axis=0)
        norm_total, bend_total = sum_rows([user_norm + time_norm, jnp.sum(bending)], n)
        relax_step = norm_total / (bend_total + damping * norm_total)
        user_factor = user_factor - relax_step * grad_user
        if sweep + 1 < SWEEPS:
            time_factor = time_factor - relax_step * grad_whole
        else:
            mine_rows = lax.dynamic_slice_in_dim(
                time_factor - relax_step * grad_whole, offset, shard_rows, 0
            )
    return (mine_rows, user_factor)


def solution(mesh):
    n = mesh.shape["user"]
    return jax.shard_map(
        lambda *args: body(n, *args),
        mesh=mesh,
        in_specs=(
            P(None, ("parts", "user")),
            P(("parts", "user")),
            P("parts", None),
            P(("parts", "user"), None),
            P(("parts", "user")),
        ),
        out_specs=(P(("parts", "user"), None), P(("parts", "user"), None)),
        check_vma=False,
    )
```

```python
import jax
import jax.numpy as jnp
from jax import lax
from jax.sharding import PartitionSpec as P

SWEEPS = 2


damping = 0.5
background = 0.5


def product(left, right, precision=lax.Precision.HIGH):
    return jnp.dot(left, right, precision=precision, preferred_element_type=jnp.float32)


def local_terms(time_factor, user_block, base_block, count_block, observed):
    linear = product(time_factor, user_block.T) + base_block[None, :]
    decay = jnp.exp(-jnp.abs(linear))
    intensity = jnp.maximum(linear, 0.0) + jnp.log1p(decay) + background
    gate_value = jnp.where(linear >= 0, 1.0, decay) / (1.0 + decay)
    inverse = 1.0 / intensity
    residual = jnp.where(observed, gate_value * (1.0 - count_block.astype(jnp.float32) * inverse), 0.0)
    curvature = jnp.where(observed, gate_value * gate_value * inverse, 0.0)
    return (residual, curvature)


def observed_of(counts, first_bin):
    time_bins = jnp.arange(counts.shape[0], dtype=jnp.int32)[:, None]
    return time_bins >= first_bin[None, :]


def exchange(value, n, distance):
    return lax.ppermute(value, "user", [(i, i ^ distance) for i in range(n)])


def sum_over_users(partial, n):
    me = lax.axis_index("user")
    if n == 1:
        return partial, [(partial, 0)], jnp.sum(partial * partial)
    if n & (n - 1) or partial.shape[0] % n:
        total = lax.psum(partial, "user")
        return total, [(total, 0)], jnp.where(me == 0, jnp.sum(total * total), 0.0)
    distances = []
    d = 1
    while d < n:
        distances.append(d)
        d *= 2
    halving, butterfly = distances[:2], distances[2:]
    block, offset = partial, 0
    for d in halving:
        half = block.shape[0] // 2
        upper = (me // d) % 2
        keep = lax.dynamic_slice_in_dim(block, upper * half, half, 0)
        send = lax.dynamic_slice_in_dim(block, (1 - upper) * half, half, 0)
        offset = offset + upper * half
        block = keep + exchange(send, n, d)
    for d in butterfly:
        block = block + exchange(block, n, d)
    share = jnp.where(me < 4, jnp.sum(block * block), 0.0)
    pieces = [(block, offset)]
    for level in reversed(range(len(halving))):
        d = halving[level]
        shift = (1 - 2 * ((me // d) % 2)) * (partial.shape[0] >> (level + 1))
        pieces = pieces + [(exchange(piece, n, d), first + shift) for piece, first in pieces]
    block = jnp.zeros_like(partial)
    for piece, first in pieces:
        block = lax.dynamic_update_slice_in_dim(block, piece, first, 0)
    return block, pieces, share


def sum_rows(values, n):
    row = lax.broadcasted_iota(jnp.int32, (n, len(values), 128), 1)
    spread = jnp.zeros(row.shape, jnp.float32)
    for k, v in enumerate(values):
        spread = jnp.where(row == k, v, spread)
    if n > 1:
        spread = lax.all_to_all(spread, "user", 0, 0, tiled=False)
    total = jnp.sum(spread, axis=0)
    return [total[k:k + 1] for k in range(len(values))]


def body(n, counts, first_bin, time_factor, user_factor, user_base):
    shard_rows = time_factor.shape[0] // n
    offset = lax.axis_index("user") * shard_rows
    mine_rows = time_factor
    observed = observed_of(counts, first_bin)
    for sweep in range(SWEEPS):
        residual, curvature = local_terms(time_factor, user_factor, user_base, counts, observed)
        if sweep + 1 < SWEEPS:
            code = lax.optimization_barrier(jnp.where(observed, counts, -1).astype(jnp.int8))
        grad_user = product(residual.T, time_factor)
        grad_whole, pieces, time_norm = sum_over_users(product(residual, user_factor), n)
        user_norm = jnp.sum(grad_user * grad_user)
        bending = jnp.zeros((user_factor.shape[0],), jnp.float32)
        for piece, first in pieces:
            rows = piece.shape[0]
            tangent_image = product(piece, user_factor.T) + product(
                lax.dynamic_slice_in_dim(time_factor, first, rows, 0), grad_user.T
            )
            weight = lax.dynamic_slice_in_dim(curvature, first, rows, 0)
            bending = bending + jnp.sum(weight * tangent_image * tangent_image, axis=0)
        norm_total, bend_total = sum_rows([user_norm + time_norm, jnp.sum(bending)], n)
        relax_step = norm_total / (bend_total + damping * norm_total)
        user_factor = user_factor - relax_step * grad_user
        if sweep + 1 < SWEEPS:
            time_factor = time_factor - relax_step * grad_whole
            counts, observed = code, code >= 0
        else:
            mine_rows = lax.dynamic_slice_in_dim(
                time_factor - relax_step * grad_whole, offset, shard_rows, 0
            )
    return (mine_rows, user_factor)


def solution(mesh):
    n = mesh.shape["user"]
    return jax.shard_map(
        lambda *args: body(n, *args),
        mesh=mesh,
        in_specs=(
            P(None, ("parts", "user")),
            P(("parts", "user")),
            P("parts", None),
            P(("parts", "user"), None),
            P(("parts", "user")),
        ),
        out_specs=(P(("parts", "user"), None), P(("parts", "user"), None)),
        check_vma=False,
    )
```

```python
import jax
import jax.numpy as jnp
from jax import lax
from jax.sharding import PartitionSpec as P

SWEEPS = 2


damping = 0.5
background = 0.5


def product(left, right, precision=lax.Precision.HIGH):
    return jnp.dot(left, right, precision=precision, preferred_element_type=jnp.float32)


def local_terms(time_factor, user_block, base_block, count_block, start_block):
    linear = product(time_factor, user_block.T) + base_block[None, :]
    time_bins = jnp.arange(time_factor.shape[0], dtype=jnp.int32)[:, None]
    observed = time_bins >= start_block[None, :]
    decay = jnp.exp(-jnp.abs(linear))
    intensity = jnp.maximum(linear, 0.0) + jnp.log1p(decay) + background
    gate_value = jnp.where(linear >= 0, 1.0, decay) / (1.0 + decay)
    inverse = 1.0 / intensity
    residual = jnp.where(observed, gate_value * (1.0 - count_block.astype(jnp.float32) * inverse), 0.0)
    curvature = jnp.where(observed, gate_value * gate_value * inverse, 0.0)
    return (residual, curvature)


def exchange(value, n, distance):
    return lax.ppermute(value, "user", [(i, i ^ distance) for i in range(n)])


def sum_over_users(partial, n):
    me = lax.axis_index("user")
    if n == 1:
        return partial, [(partial, 0)], jnp.sum(partial * partial)
    if n & (n - 1) or partial.shape[0] % n:
        total = lax.psum(partial, "user")
        return total, [(total, 0)], jnp.where(me == 0, jnp.sum(total * total), 0.0)
    distances = []
    d = 1
    while d < n:
        distances.append(d)
        d *= 2
    halving, butterfly = distances[:2], distances[2:]
    block, offset = partial, 0
    for d in halving:
        half = block.shape[0] // 2
        upper = (me // d) % 2
        keep = lax.dynamic_slice_in_dim(block, upper * half, half, 0)
        send = lax.dynamic_slice_in_dim(block, (1 - upper) * half, half, 0)
        offset = offset + upper * half
        block = keep + exchange(send, n, d)
    for d in butterfly:
        block = block + exchange(block, n, d)
    share = jnp.where(me < 4, jnp.sum(block * block), 0.0)
    pieces = [(block, offset)]
    for level in reversed(range(len(halving))):
        d = halving[level]
        shift = (1 - 2 * ((me // d) % 2)) * (partial.shape[0] >> (level + 1))
        pieces = pieces + [(exchange(piece, n, d), first + shift) for piece, first in pieces]
    block = jnp.zeros_like(partial)
    for piece, first in pieces:
        block = lax.dynamic_update_slice_in_dim(block, piece, first, 0)
    return block, pieces, share


def sum_rows(values, n):
    row = lax.broadcasted_iota(jnp.int32, (n, len(values), 128), 1)
    spread = jnp.zeros(row.shape, jnp.float32)
    for k, v in enumerate(values):
        spread = jnp.where(row == k, v, spread)
    if n > 1:
        spread = lax.all_to_all(spread, "user", 0, 0, tiled=False)
    total = jnp.sum(spread, axis=0)
    return [total[k:k + 1] for k in range(len(values))]


def body(n, counts, first_bin, time_factor, user_factor, user_base):
    shard_rows = time_factor.shape[0] // n
    offset = lax.axis_index("user") * shard_rows
    mine_rows = time_factor
    for sweep in range(SWEEPS):
        residual, curvature = local_terms(time_factor, user_factor, user_base, counts, first_bin)
        grad_user = product(residual.T, time_factor)
        grad_whole, pieces, time_norm = sum_over_users(product(residual, user_factor), n)
        user_norm = jnp.sum(grad_user * grad_user)
        bending = jnp.zeros((user_factor.shape[0],), jnp.float32)
        for piece, first in pieces:
            rows = piece.shape[0]
            tangent_image = product(piece, user_factor.T) + product(
                lax.dynamic_slice_in_dim(time_factor, first, rows, 0), grad_user.T
            )
            weight = lax.dynamic_slice_in_dim(curvature, first, rows, 0)
            bending = bending + jnp.sum(weight * tangent_image * tangent_image, axis=0)
        lanes = jnp.sum(bending.reshape(-1, 128), axis=0)
        norm_total, bend_lanes = sum_rows([user_norm + time_norm, lanes], n)
        bend_total = jnp.sum(bend_lanes, axis=1, keepdims=True)
        relax_step = norm_total / (bend_total + damping * norm_total)
        user_factor = user_factor - relax_step * grad_user
        if sweep + 1 < SWEEPS:
            time_factor = time_factor - relax_step * grad_whole
        else:
            mine_rows = lax.dynamic_slice_in_dim(
                time_factor - relax_step * grad_whole, offset, shard_rows, 0
            )
    return (mine_rows, user_factor)


def solution(mesh):
    n = mesh.shape["user"]
    return jax.shard_map(
        lambda *args: body(n, *args),
        mesh=mesh,
        in_specs=(
            P(None, ("parts", "user")),
            P(("parts", "user")),
            P("parts", None),
            P(("parts", "user"), None),
            P(("parts", "user")),
        ),
        out_specs=(P(("parts", "user"), None), P(("parts", "user"), None)),
        check_vma=False,
    )
```

```python
import jax
import jax.numpy as jnp
from jax import lax
from jax.sharding import PartitionSpec as P

SWEEPS = 2


damping = 0.5
background = 0.5


def product(left, right, precision=lax.Precision.HIGH):
    return jnp.dot(left, right, precision=precision, preferred_element_type=jnp.float32)


def local_terms(time_factor, user_block, base_block, count_block, start_block):
    linear = product(time_factor, user_block.T) + base_block[None, :]
    time_bins = jnp.arange(time_factor.shape[0], dtype=jnp.int32)[:, None]
    observed = time_bins >= start_block[None, :]
    decay = jnp.exp(-jnp.abs(linear))
    intensity = jnp.maximum(linear, 0.0) + jnp.log1p(decay) + background
    gate_value = jnp.where(linear >= 0, 1.0, decay) / (1.0 + decay)
    inverse = 1.0 / intensity
    residual = jnp.where(observed, gate_value * (1.0 - count_block.astype(jnp.float32) * inverse), 0.0)
    curvature = jnp.where(observed, gate_value * gate_value * inverse, 0.0)
    return (residual, curvature)


def exchange(value, n, distance):
    return lax.ppermute(value, "user", [(i, i ^ distance) for i in range(n)])


def sum_over_users(partial, n):
    me = lax.axis_index("user")
    if n == 1:
        return partial, [(partial, 0)], jnp.sum(partial * partial)
    if n & (n - 1) or partial.shape[0] % n:
        total = lax.psum(partial, "user")
        return total, [(total, 0)], jnp.where(me == 0, jnp.sum(total * total), 0.0)
    distances = []
    d = 1
    while d < n:
        distances.append(d)
        d *= 2
    halving, butterfly = distances[:2], distances[2:]
    block, offset = partial, 0
    for d in halving:
        half = block.shape[0] // 2
        upper = (me // d) % 2
        keep = lax.dynamic_slice_in_dim(block, upper * half, half, 0)
        send = lax.dynamic_slice_in_dim(block, (1 - upper) * half, half, 0)
        offset = offset + upper * half
        block = keep + exchange(send, n, d)
    for d in butterfly:
        block = block + exchange(block, n, d)
    share = jnp.where(me < 4, jnp.sum(block * block), 0.0)
    pieces = [(block, offset)]
    rows = block.shape[0]
    for level in reversed(range(len(halving))):
        d = halving[level]
        shift = (1 - 2 * ((me // d) % 2)) * (partial.shape[0] >> (level + 1))
        held = jnp.concatenate([piece for piece, _ in pieces]) if len(pieces) > 1 else pieces[0][0]
        got = exchange(held, n, d)
        pieces = pieces + [(got[k * rows:(k + 1) * rows], first + shift) for k, (_, first) in enumerate(pieces)]
    block = jnp.zeros_like(partial)
    for piece, first in pieces:
        block = lax.dynamic_update_slice_in_dim(block, piece, first, 0)
    return block, pieces, share


def sum_rows(values, n):
    row = lax.broadcasted_iota(jnp.int32, (n, len(values), 128), 1)
    spread = jnp.zeros(row.shape, jnp.float32)
    for k, v in enumerate(values):
        spread = jnp.where(row == k, v, spread)
    if n > 1:
        spread = lax.all_to_all(spread, "user", 0, 0, tiled=False)
    total = jnp.sum(spread, axis=0)
    return [total[k:k + 1] for k in range(len(values))]


def body(n, counts, first_bin, time_factor, user_factor, user_base):
    shard_rows = time_factor.shape[0] // n
    offset = lax.axis_index("user") * shard_rows
    mine_rows = time_factor
    for sweep in range(SWEEPS):
        residual, curvature = local_terms(time_factor, user_factor, user_base, counts, first_bin)
        grad_user = product(residual.T, time_factor)
        grad_whole, pieces, time_norm = sum_over_users(product(residual, user_factor), n)
        user_norm = jnp.sum(grad_user * grad_user)
        bending = jnp.zeros((user_factor.shape[0],), jnp.float32)
        for piece, first in pieces:
            rows = piece.shape[0]
            tangent_image = product(piece, user_factor.T) + product(
                lax.dynamic_slice_in_dim(time_factor, first, rows, 0), grad_user.T
            )
            weight = lax.dynamic_slice_in_dim(curvature, first, rows, 0)
            bending = bending + jnp.sum(weight * tangent_image * tangent_image, axis=0)
        lanes = jnp.sum(bending.reshape(-1, 128), axis=0)
        norm_total, bend_lanes = sum_rows([user_norm + time_norm, lanes], n)
        bend_total = jnp.sum(bend_lanes, axis=1, keepdims=True)
        relax_step = norm_total / (bend_total + damping * norm_total)
        user_factor = user_factor - relax_step * grad_user
        if sweep + 1 < SWEEPS:
            time_factor = time_factor - relax_step * grad_whole
        else:
            mine_rows = lax.dynamic_slice_in_dim(
                time_factor - relax_step * grad_whole, offset, shard_rows, 0
            )
    return (mine_rows, user_factor)


def solution(mesh):
    n = mesh.shape["user"]
    return jax.shard_map(
        lambda *args: body(n, *args),
        mesh=mesh,
        in_specs=(
            P(None, ("parts", "user")),
            P(("parts", "user")),
            P("parts", None),
            P(("parts", "user"), None),
            P(("parts", "user")),
        ),
        out_specs=(P(("parts", "user"), None), P(("parts", "user"), None)),
        check_vma=False,
    )
```

```python
import jax
import jax.numpy as jnp
from jax import lax
from jax.sharding import PartitionSpec as P

SWEEPS = 2


damping = 0.5
background = 0.5


def product(left, right, precision=lax.Precision.HIGH):
    return jnp.dot(left, right, precision=precision, preferred_element_type=jnp.float32)


def local_terms(time_factor, user_block, base_block, count_block, start_block):
    linear = product(time_factor, user_block.T) + base_block[None, :]
    time_bins = jnp.arange(time_factor.shape[0], dtype=jnp.int32)[:, None]
    observed = time_bins >= start_block[None, :]
    decay = jnp.exp(-jnp.abs(linear))
    intensity = jnp.maximum(linear, 0.0) + jnp.log1p(decay) + background
    gate_value = jnp.where(linear >= 0, 1.0, decay) / (1.0 + decay)
    inverse = 1.0 / intensity
    residual = jnp.where(observed, gate_value * (1.0 - count_block.astype(jnp.float32) * inverse), 0.0)
    curvature = jnp.where(observed, gate_value * gate_value * inverse, 0.0)
    return (residual, curvature)


def exchange(value, n, distance):
    return lax.ppermute(value, "user", [(i, i ^ distance) for i in range(n)])


def sum_over_users(partial, n):
    me = lax.axis_index("user")
    if n == 1:
        return partial, [(partial, 0)], jnp.sum(partial * partial, axis=0)
    if n & (n - 1) or partial.shape[0] % n:
        total = lax.psum(partial, "user")
        return total, [(total, 0)], jnp.where(me == 0, jnp.sum(total * total, axis=0), 0.0)
    distances = []
    d = 1
    while d < n:
        distances.append(d)
        d *= 2
    halving, butterfly = distances[:2], distances[2:]
    block, offset = partial, 0
    for d in halving:
        half = block.shape[0] // 2
        upper = (me // d) % 2
        keep = lax.dynamic_slice_in_dim(block, upper * half, half, 0)
        send = lax.dynamic_slice_in_dim(block, (1 - upper) * half, half, 0)
        offset = offset + upper * half
        block = keep + exchange(send, n, d)
    for d in butterfly:
        block = block + exchange(block, n, d)
    share = jnp.where(me < 4, jnp.sum(block * block, axis=0), 0.0)
    pieces = [(block, offset)]
    for level in reversed(range(len(halving))):
        d = halving[level]
        shift = (1 - 2 * ((me // d) % 2)) * (partial.shape[0] >> (level + 1))
        pieces = pieces + [(exchange(piece, n, d), first + shift) for piece, first in pieces]
    block = jnp.zeros_like(partial)
    for piece, first in pieces:
        block = lax.dynamic_update_slice_in_dim(block, piece, first, 0)
    return block, pieces, share


def sum_rows(values, n):
    row = lax.broadcasted_iota(jnp.int32, (n, len(values), 128), 1)
    spread = jnp.zeros(row.shape, jnp.float32)
    for k, v in enumerate(values):
        spread = jnp.where(row == k, v, spread)
    if n > 1:
        spread = lax.all_to_all(spread, "user", 0, 0, tiled=False)
    total = jnp.sum(spread, axis=0)
    return [total[k:k + 1] for k in range(len(values))]


def body(n, counts, first_bin, time_factor, user_factor, user_base):
    shard_rows = time_factor.shape[0] // n
    offset = lax.axis_index("user") * shard_rows
    mine_rows = time_factor
    for sweep in range(SWEEPS):
        residual, curvature = local_terms(time_factor, user_factor, user_base, counts, first_bin)
        grad_user = product(residual.T, time_factor)
        grad_whole, pieces, time_norm = sum_over_users(product(residual, user_factor), n)
        user_norm = jnp.sum(grad_user * grad_user, axis=0)
        bending = jnp.zeros((user_factor.shape[0],), jnp.float32)
        for piece, first in pieces:
            rows = piece.shape[0]
            tangent_image = product(piece, user_factor.T) + product(
                lax.dynamic_slice_in_dim(time_factor, first, rows, 0), grad_user.T
            )
            weight = lax.dynamic_slice_in_dim(curvature, first, rows, 0)
            bending = bending + jnp.sum(weight * tangent_image * tangent_image, axis=0)
        lanes = jnp.sum(bending.reshape(-1, 128), axis=0)
        norm_lanes, bend_lanes = sum_rows([user_norm + time_norm, lanes], n)
        norm_total = jnp.sum(norm_lanes, axis=1, keepdims=True)
        bend_total = jnp.sum(bend_lanes, axis=1, keepdims=True)
        relax_step = jnp.broadcast_to(norm_total / (bend_total + damping * norm_total), (1, 128))
        user_factor = user_factor - relax_step * grad_user
        if sweep + 1 < SWEEPS:
            time_factor = time_factor - relax_step * grad_whole
        else:
            mine_rows = lax.dynamic_slice_in_dim(
                time_factor - relax_step * grad_whole, offset, shard_rows, 0
            )
    return (mine_rows, user_factor)


def solution(mesh):
    n = mesh.shape["user"]
    return jax.shard_map(
        lambda *args: body(n, *args),
        mesh=mesh,
        in_specs=(
            P(None, ("parts", "user")),
            P(("parts", "user")),
            P("parts", None),
            P(("parts", "user"), None),
            P(("parts", "user")),
        ),
        out_specs=(P(("parts", "user"), None), P(("parts", "user"), None)),
        check_vma=False,
    )
```

```python
import jax
import jax.numpy as jnp
from jax import lax
from jax.sharding import PartitionSpec as P

SWEEPS = 2


damping = 0.5
background = 0.5


def product(left, right, precision=lax.Precision.HIGH):
    return jnp.dot(left, right, precision=precision, preferred_element_type=jnp.float32)


def local_terms(time_factor, user_block, base_block, count_block, start_block):
    linear = product(time_factor, user_block.T) + base_block[None, :]
    time_bins = jnp.arange(time_factor.shape[0], dtype=jnp.int32)[:, None]
    observed = time_bins >= start_block[None, :]
    decay = jnp.exp(-jnp.abs(linear))
    intensity = jnp.maximum(linear, 0.0) + jnp.log1p(decay) + background
    gate_value = jnp.where(linear >= 0, 1.0, decay) / (1.0 + decay)
    inverse = 1.0 / intensity
    residual = jnp.where(observed, gate_value * (1.0 - count_block.astype(jnp.float32) * inverse), 0.0)
    curvature = jnp.where(observed, gate_value * gate_value * inverse, 0.0)
    return (residual, curvature)


def exchange(value, n, distance):
    return lax.ppermute(value, "user", [(i, i ^ distance) for i in range(n)])


def sum_over_users(partial, n, halves=None):
    if halves is not None:
        partial = jnp.zeros((2 * halves[0].shape[0], halves[0].shape[1]), halves[0].dtype)
    me = lax.axis_index("user")
    if n == 1:
        return partial, [(partial, 0)], jnp.sum(partial * partial)
    if n & (n - 1) or partial.shape[0] % n:
        total = lax.psum(partial, "user")
        return total, [(total, 0)], jnp.where(me == 0, jnp.sum(total * total), 0.0)
    distances = []
    d = 1
    while d < n:
        distances.append(d)
        d *= 2
    halving, butterfly = distances[:2], distances[2:]
    block, offset = partial, 0
    if halves is not None:
        lower, upper_half = halves
        upper = me % 2
        from_even = lax.ppermute(upper_half, "user", [(i, i ^ 1) for i in range(0, n, 2)])
        from_odd = lax.ppermute(lower, "user", [(i, i ^ 1) for i in range(1, n, 2)])
        block = jnp.where(upper == 0, lower, upper_half) + from_even + from_odd
        offset = upper * lower.shape[0]
        halving_rest = halving[1:]
    else:
        halving_rest = halving
    for d in halving_rest:
        half = block.shape[0] // 2
        upper = (me // d) % 2
        keep = lax.dynamic_slice_in_dim(block, upper * half, half, 0)
        send = lax.dynamic_slice_in_dim(block, (1 - upper) * half, half, 0)
        offset = offset + upper * half
        block = keep + exchange(send, n, d)
    for d in butterfly:
        block = block + exchange(block, n, d)
    share = jnp.where(me < 4, jnp.sum(block * block), 0.0)
    pieces = [(block, offset)]
    for level in reversed(range(len(halving))):
        d = halving[level]
        shift = (1 - 2 * ((me // d) % 2)) * (partial.shape[0] >> (level + 1))
        pieces = pieces + [(exchange(piece, n, d), first + shift) for piece, first in pieces]
    block = jnp.zeros_like(partial)
    for piece, first in pieces:
        block = lax.dynamic_update_slice_in_dim(block, piece, first, 0)
    return block, pieces, share


def sum_rows(values, n):
    row = lax.broadcasted_iota(jnp.int32, (n, len(values), 128), 1)
    spread = jnp.zeros(row.shape, jnp.float32)
    for k, v in enumerate(values):
        spread = jnp.where(row == k, v, spread)
    if n > 1:
        spread = lax.all_to_all(spread, "user", 0, 0, tiled=False)
    total = jnp.sum(spread, axis=0)
    return [total[k:k + 1] for k in range(len(values))]


def body(n, counts, first_bin, time_factor, user_factor, user_base):
    shard_rows = time_factor.shape[0] // n
    offset = lax.axis_index("user") * shard_rows
    mine_rows = time_factor
    for sweep in range(SWEEPS):
        residual, curvature = local_terms(time_factor, user_factor, user_base, counts, first_bin)
        grad_user = product(residual.T, time_factor)
        half = residual.shape[0] // 2
        grad_whole, pieces, time_norm = sum_over_users(
            None, n, (product(residual[:half], user_factor), product(residual[half:], user_factor))
        ) if n >= 4 and not n & (n - 1) and residual.shape[0] % n == 0 else sum_over_users(
            product(residual, user_factor), n
        )
        user_norm = jnp.sum(grad_user * grad_user)
        bending = jnp.zeros((user_factor.shape[0],), jnp.float32)
        for piece, first in pieces:
            rows = piece.shape[0]
            tangent_image = product(piece, user_factor.T) + product(
                lax.dynamic_slice_in_dim(time_factor, first, rows, 0), grad_user.T
            )
            weight = lax.dynamic_slice_in_dim(curvature, first, rows, 0)
            bending = bending + jnp.sum(weight * tangent_image * tangent_image, axis=0)
        lanes = jnp.sum(bending.reshape(-1, 128), axis=0)
        norm_total, bend_lanes = sum_rows([user_norm + time_norm, lanes], n)
        bend_total = jnp.sum(bend_lanes, axis=1, keepdims=True)
        relax_step = norm_total / (bend_total + damping * norm_total)
        user_factor = user_factor - relax_step * grad_user
        if sweep + 1 < SWEEPS:
            time_factor = time_factor - relax_step * grad_whole
        else:
            mine_rows = lax.dynamic_slice_in_dim(
                time_factor - relax_step * grad_whole, offset, shard_rows, 0
            )
    return (mine_rows, user_factor)


def solution(mesh):
    n = mesh.shape["user"]
    return jax.shard_map(
        lambda *args: body(n, *args),
        mesh=mesh,
        in_specs=(
            P(None, ("parts", "user")),
            P(("parts", "user")),
            P("parts", None),
            P(("parts", "user"), None),
            P(("parts", "user")),
        ),
        out_specs=(P(("parts", "user"), None), P(("parts", "user"), None)),
        check_vma=False,
    )
```

```python
import jax
import jax.numpy as jnp
from jax import lax
from jax.sharding import PartitionSpec as P

SWEEPS = 2


damping = 0.5
background = 0.5


def product(left, right, precision=lax.Precision.HIGH):
    return jnp.dot(left, right, precision=precision, preferred_element_type=jnp.float32)


def local_terms(time_factor, user_block, base_block, count_block, start_block):
    linear = product(time_factor, user_block.T) + base_block[None, :]
    time_bins = jnp.arange(time_factor.shape[0], dtype=jnp.int32)[:, None]
    observed = time_bins >= start_block[None, :]
    decay = jnp.exp(-jnp.abs(linear))
    intensity = jnp.maximum(linear, 0.0) + jnp.log1p(decay) + background
    gate_value = jnp.where(linear >= 0, 1.0, decay) / (1.0 + decay)
    inverse = 1.0 / intensity
    residual = jnp.where(observed, gate_value * (1.0 - count_block.astype(jnp.float32) * inverse), 0.0)
    curvature = jnp.where(observed, gate_value * gate_value * inverse, 0.0)
    return (residual, curvature)


def exchange(value, n, distance):
    return lax.ppermute(value, "user", [(i, i ^ distance) for i in range(n)])


def sum_over_users(partial, n):
    me = lax.axis_index("user")
    if n == 1:
        return partial, [(partial, 0)], jnp.sum(partial * partial)
    if n & (n - 1) or partial.shape[0] % n:
        total = lax.psum(partial, "user")
        return total, [(total, 0)], jnp.where(me == 0, jnp.sum(total * total), 0.0)
    distances = []
    d = 1
    while d < n:
        distances.append(d)
        d *= 2
    halving, butterfly = distances[:2], distances[2:]
    block, offset = partial, 0
    for d in halving:
        half = block.shape[0] // 2
        upper = (me // d) % 2
        keep = lax.dynamic_slice_in_dim(block, upper * half, half, 0)
        send = lax.dynamic_slice_in_dim(block, (1 - upper) * half, half, 0)
        offset = offset + upper * half
        block = keep + exchange(send, n, d)
    for d in butterfly:
        block = block + exchange(block, n, d)
    share = jnp.where(me < 4, jnp.sum(block * block), 0.0)
    pieces = [(block, offset)]
    for level in reversed(range(len(halving))):
        d = halving[level]
        shift = (1 - 2 * ((me // d) % 2)) * (partial.shape[0] >> (level + 1))
        pieces = pieces + [(exchange(piece, n, d), first + shift) for piece, first in pieces]
    block = jnp.zeros_like(partial)
    for piece, first in pieces:
        block = lax.dynamic_update_slice_in_dim(block, piece, first, 0)
    return block, pieces, share


def sum_rows(values, n):
    row = lax.broadcasted_iota(jnp.int32, (n, len(values), 128), 1)
    spread = jnp.zeros(row.shape, jnp.float32)
    for k, v in enumerate(values):
        spread = jnp.where(row == k, v, spread)
    if n > 1:
        spread = lax.all_to_all(spread, "user", 0, 0, tiled=False)
    total = jnp.sum(spread, axis=0)
    return [total[k:k + 1] for k in range(len(values))]


def body(n, counts, first_bin, time_factor, user_factor, user_base):
    shard_rows = time_factor.shape[0] // n
    offset = lax.axis_index("user") * shard_rows
    mine_rows = time_factor
    for sweep in range(SWEEPS):
        residual, curvature = local_terms(time_factor, user_factor, user_base, counts, first_bin)
        grad_user = product(residual.T, time_factor)
        grad_whole, pieces, time_norm = sum_over_users(product(residual, user_factor), n)
        user_norm = jnp.sum(grad_user * grad_user)
        bending = jnp.zeros((user_factor.shape[0],), jnp.float32)
        for piece, first in pieces:
            rows = piece.shape[0]
            tangent_image = product(piece, user_factor.T) + product(
                lax.dynamic_slice_in_dim(time_factor, first, rows, 0), grad_user.T
            )
            weight = lax.dynamic_slice_in_dim(curvature, first, rows, 0)
            bending = bending + jnp.sum(weight * tangent_image * tangent_image, axis=0)
        lanes = jnp.sum(bending.reshape(-1, 128), axis=0)
        norm_total, bend_lanes = sum_rows([user_norm + time_norm, lanes], n)
        bend_total = jnp.dot(bend_lanes, jnp.ones((128, 128), jnp.float32), precision=lax.Precision.HIGHEST)
        relax_step = norm_total / (bend_total + damping * norm_total)
        user_factor = user_factor - relax_step * grad_user
        if sweep + 1 < SWEEPS:
            time_factor = time_factor - relax_step * grad_whole
        else:
            mine_rows = lax.dynamic_slice_in_dim(
                time_factor - relax_step * grad_whole, offset, shard_rows, 0
            )
    return (mine_rows, user_factor)


def solution(mesh):
    n = mesh.shape["user"]
    return jax.shard_map(
        lambda *args: body(n, *args),
        mesh=mesh,
        in_specs=(
            P(None, ("parts", "user")),
            P(("parts", "user")),
            P("parts", None),
            P(("parts", "user"), None),
            P(("parts", "user")),
        ),
        out_specs=(P(("parts", "user"), None), P(("parts", "user"), None)),
        check_vma=False,
    )
```
